32 devices in a mesh: clips: 2 (over y), space: 8 (over z, x), tm: 2 (over core).
Axes of the slice: x: 2, y: 2, z: 4, core: 2. Of those that a mesh axis runs over, the one named last changes fastest.
Arguments:
- frames: bfloat16 [2, 2, 16, 112, 192], P('clips', 'tm', 'space'), parts along dimension 0, may hold values from -100 to 100
- norm1_gain: float32 [192], replicated, may hold values from 0.1 to 1.9
- conv1_weight: bfloat16 [3, 3, 3, 192, 192], replicated, may hold values from -0.078125 to 0.078125
- conv1_bias: float32 [192], replicated, may hold values from -3 to 3
- norm2_gain: float32 [192], replicated, may hold values from 0.1 to 1.9
- conv2_weight: bfloat16 [3, 3, 3, 192, 192], replicated, may hold values from -0.078125 to 0.078125
- conv2_bias: float32 [192], replicated, may hold values from -3 to 3
- attn_gain: float32 [192], replicated, may hold values from 0.5 to 3
- w_query: bfloat16 [192, 192], replicated, may hold values from -3 to 3
- b_query: float32 [192], replicated, may hold values from -4 to 4
- w_key: bfloat16 [192, 192], replicated, may hold values from -1 to 2
- w_value: bfloat16 [192, 192], replicated, may hold values from -0.4375 to 0.4375
- b_value: float32 [192], replicated, may hold values from -3 to 3
- w_out: bfloat16 [192, 192], replicated, may hold values from -0.4375 to 0.4375
- b_out: float32 [192], replicated, may hold values from -3 to 3
Outputs:
- decoded: float32 [2, 2, 16, 112, 192], P('clips', 'tm', 'space'), parts along dimension 0
The draws below stay inside these ranges and needn't reach their ends.
There are 2 independent parts, one for each index of `clips`. The reference program is written for one: setup_inputs(seed, part) draws one part's arguments, and reference() takes and returns one part's arrays. A program takes and returns all parts, laid end to end along the dimension named above; an argument that names none is the same for every part. Nothing has to cross between parts.
All inputs are finite; a program needn't handle non-finite values.
Results may differ from the reference program's by a relative error of at most 0.02.
Values may be sent and summed in bfloat16 or wider, within the bound.
No kernel may reach another device: no remote copies, remote signals or barrier semaphores. Data moves between devices by JAX's collectives and lax.ppermute only.
A program may use at most 128 MiB of HBM per device.

```python
import math
import jax
import jax.numpy as jnp
from jax import lax

C = 192
COLS = 112
FR_DEV = 1
HEIGHT = 16
N_TM = 2


def draw_frames(key, part):
    shape = (FR_DEV, N_TM, HEIGHT, COLS, C)
    keys_list = jax.random.split(jax.random.fold_in(key, 5), 1)
    base = jax.random.normal(keys_list[0], shape, jnp.float32)
    return jnp.clip(base, -6.0, 6.0).astype(jnp.bfloat16)


def draw_attn_gain(key, part):
    gain_key = jax.random.fold_in(key, 37)
    return jax.random.uniform(gain_key, (C,), jnp.float32, 0.7, 1.3)


def draw_w_query(key, part):
    query_key = jax.random.fold_in(key, 11)
    noise = jnp.clip(jax.random.normal(query_key, (C, C), jnp.float32), -4.0, 4.0) / math.sqrt(C)
    return jnp.clip(3.0 * noise, -3.0, 3.0).astype(jnp.bfloat16)


def draw_w_key(key, part):
    key_key = jax.random.fold_in(key, 23)
    noise = jnp.clip(jax.random.normal(key_key, (C, C), jnp.float32), -4.0, 4.0) / math.sqrt(C)
    return jnp.clip(noise, -1.0, 1.0).astype(jnp.bfloat16)


def centred(rng, shape, width, reach, held_as=jnp.bfloat16):
    values = width * jax.random.normal(rng, shape, jnp.float32)
    return jnp.clip(values, min=-reach, max=reach).astype(held_as)


def setup_inputs(seed: int = 0, part: int = 0) -> dict:
    seeds = jax.random.split(jax.random.key(seed), 16)
    part_keys = jax.random.split(jax.random.fold_in(seeds[15], part), 16)
    frames = draw_frames(jax.random.fold_in(jax.random.fold_in(seeds[15], part), 71), part)
    norm1_gain = jnp.clip(1.0 + 0.18 * jax.random.normal(seeds[1], (C,), jnp.float32), 0.1, 1.9)
    conv1_weight = centred(seeds[2], (3, 3, 3, C, C), (27 * C) ** -0.5, 0.078125)
    conv1_bias = centred(seeds[3], (C,), 0.5, 3.0, jnp.float32)
    norm2_gain = jnp.clip(1.0 + 0.18 * jax.random.normal(seeds[4], (C,), jnp.float32), 0.1, 1.9)
    conv2_weight = centred(seeds[5], (3, 3, 3, C, C), (27 * C) ** -0.5, 0.078125)
    conv2_bias = centred(seeds[6], (C,), 0.5, 3.0, jnp.float32)
    attn_gain = draw_attn_gain(jax.random.fold_in(seeds[15], 71), part)
    w_query = draw_w_query(jax.random.fold_in(seeds[15], 71), part)
    b_query = centred(seeds[9], (C,), 1.0, 4.0, jnp.float32)
    w_key = draw_w_key(jax.random.fold_in(seeds[15], 71), part)
    w_value = centred(seeds[11], (C, C), C ** -0.5, 0.4375)
    b_value = centred(seeds[12], (C,), 0.5, 3.0, jnp.float32)
    w_out = centred(seeds[13], (C, C), C ** -0.5, 0.4375)
    b_out = centred(seeds[14], (C,), 0.5, 3.0, jnp.float32)
    return {"frames": frames, "norm1_gain": norm1_gain, "conv1_weight": conv1_weight, "conv1_bias": conv1_bias, "norm2_gain": norm2_gain, "conv2_weight": conv2_weight, "conv2_bias": conv2_bias, "attn_gain": attn_gain, "w_query": w_query, "b_query": b_query, "w_key": w_key, "w_value": w_value, "b_value": b_value, "w_out": w_out, "b_out": b_out}


epsilon = 1e-06

def rms_scale(values, gain):
    return values * lax.rsqrt(lax.optimization_barrier(jnp.mean(values * values, axis=-1, keepdims=True)) + epsilon) * gain

def causal_conv(inputs, weight, bias):
    frame_count, row_count, col_count, channels = inputs.shape
    padded = jnp.pad(inputs, ((2, 0), (1, 1), (1, 1), (0, 0)))
    summed = jnp.zeros((frame_count * row_count * col_count, channels), jnp.float32)
    for t in range(3):
        for r in range(3):
            for c in range(3):
                window = padded[t:t + frame_count, r:r + row_count, c:c + col_count].reshape(-1, channels)
                summed = summed + jnp.dot(window, weight[t, r, c], preferred_element_type=jnp.float32)
    return summed.reshape(frame_count, row_count, col_count, channels) + bias

def attend_frame(operands):
    frame_queries, frame_keys = operands
    token_count, channels = frame_keys.shape
    block_rows = math.gcd(token_count, 1024)
    blocks = frame_queries.reshape(token_count // block_rows, block_rows, channels)

    def one_block(query_block):
        scores = jnp.dot(query_block, frame_keys.T, preferred_element_type=jnp.float32)
        highest = lax.optimization_barrier(jnp.max(scores, axis=-1, keepdims=True))
        weights = jnp.exp(scores - highest)
        total = lax.optimization_barrier(jnp.sum(weights, axis=-1, keepdims=True))
        numer = jnp.dot(weights.astype(jnp.bfloat16), frame_keys, preferred_element_type=jnp.float32)
        return (numer / total).astype(jnp.bfloat16)
    return lax.map(one_block, blocks).reshape(token_count, channels)

def reference(frames, norm1_gain, conv1_weight, conv1_bias, norm2_gain, conv2_weight, conv2_bias, attn_gain, w_query, b_query, w_key, w_value, b_value, w_out, b_out):
    shape_all = frames.shape
    frame_total = shape_all[0] * shape_all[1]
    row_count, col_count, channels = (shape_all[2], shape_all[3], shape_all[4])
    frame_values = frames.reshape(frame_total, row_count, col_count, channels).astype(jnp.float32)
    first_act = jax.nn.silu(rms_scale(frame_values, norm1_gain)).astype(jnp.bfloat16)
    first_out = causal_conv(first_act, conv1_weight, conv1_bias)
    second_act = jax.nn.silu(rms_scale(first_out, norm2_gain)).astype(jnp.bfloat16)
    second_out = causal_conv(second_act, conv2_weight, conv2_bias)
    residual = frame_values + second_out
    normed = rms_scale(residual, attn_gain).astype(jnp.bfloat16)
    flat = normed.reshape(-1, channels)
    query = (jnp.dot(flat, w_query, preferred_element_type=jnp.float32) + b_query).astype(jnp.bfloat16)
    folded = (jnp.dot(query, w_key.T, preferred_element_type=jnp.float32) * (1.0 / math.sqrt(channels))).astype(jnp.bfloat16)
    token_count = row_count * col_count
    mixed = lax.map(attend_frame, (folded.reshape(frame_total, token_count, channels), flat.reshape(frame_total, token_count, channels)))
    value = (jnp.dot(mixed.reshape(-1, channels), w_value, preferred_element_type=jnp.float32) + b_value).astype(jnp.bfloat16)
    decoded = residual.reshape(-1, channels) + jnp.dot(value, w_out, preferred_element_type=jnp.float32) + b_out
    return decoded.reshape(shape_all)
```

```python
import math

import jax
import jax.numpy as jnp
from jax import lax
from jax.sharding import PartitionSpec as P

epsilon = 1e-06
HALO = 2


def rms_scale(values, gain):
    return values * lax.rsqrt(jnp.mean(values * values, axis=-1, keepdims=True) + epsilon) * gain


def conv_rows(source, taps):
    return lax.conv_general_dilated(
        source,
        taps,
        window_strides=(1, 1),
        padding=((0, 0), (1, 1)),
        dimension_numbers=("NHWC", "HWIO", "NHWC"),
        preferred_element_type=jnp.float32,
    )


def causal_time_conv(seq, weight):
    frame_total = seq.shape[0]
    out = None
    for p in range(3):
        lag = 2 - p
        if lag >= frame_total:
            continue
        part = conv_rows(seq[: frame_total - lag], weight[p])
        if lag:
            part = jnp.pad(part, ((lag, 0), (0, 0), (0, 0), (0, 0)))
        out = part if out is None else out + part
    return out


def local(
    frames,
    norm1_gain,
    conv1_weight,
    conv1_bias,
    norm2_gain,
    conv2_weight,
    conv2_bias,
    attn_gain,
    w_query,
    b_query,
    w_key,
    w_value,
    b_value,
    w_out,
    b_out,
):
    own = frames[:, 0]
    frame_count, row_count, col_count, channels = own.shape
    bands = lax.axis_size("space")
    band = lax.axis_index("space")
    is_first = lax.axis_index("tm") == 0
    height = bands * row_count

    partner = lax.ppermute(own, "tm", [(0, 1), (1, 0)])
    even = jnp.where(is_first, own, partner)
    odd = jnp.where(is_first, partner, own)
    seq = jnp.stack([even, odd], axis=1).reshape(2 * frame_count, row_count, col_count, channels)

    up = [(i, i + 1) for i in range(bands - 1)]
    down = [(i + 1, i) for i in range(bands - 1)]
    above = lax.ppermute(seq[:, row_count - HALO :], "space", up)
    below = lax.ppermute(seq[:, :HALO], "space", down)
    ext = jnp.concatenate([above, seq, below], axis=1)

    first_act = jax.nn.silu(rms_scale(ext.astype(jnp.float32), norm1_gain)).astype(jnp.bfloat16)
    first_out = causal_time_conv(first_act, conv1_weight) + conv1_bias
    rows = band * row_count - 1 + lax.broadcasted_iota(jnp.int32, (1, row_count + 2, 1, 1), 1)
    inside = (rows >= 0) & (rows < height)
    second_act = jnp.where(
        inside, jax.nn.silu(rms_scale(first_out, norm2_gain)), 0.0
    ).astype(jnp.bfloat16)

    pairs = second_act.reshape(frame_count, 2, row_count + 2, col_count, channels)
    sa_even = pairs[:, 0]
    sa_odd = pairs[:, 1]
    zero = jnp.zeros_like(sa_even[:1])
    odd_before = jnp.concatenate([zero, sa_odd[:-1]], axis=0)
    even_before = jnp.concatenate([zero, sa_even[:-1]], axis=0)
    current = jnp.where(is_first, sa_even, sa_odd)
    previous = jnp.where(is_first, odd_before, sa_even)
    second_out = conv_rows(current, conv2_weight[2]) + conv_rows(previous, conv2_weight[1])
    if frame_count > 1:
        oldest = jnp.where(is_first, even_before, odd_before)
        second_out = second_out + conv_rows(oldest, conv2_weight[0])
    second_out = second_out + conv2_bias

    frame_values = own.astype(jnp.float32)
    residual = frame_values + second_out
    normed = rms_scale(residual, attn_gain).astype(jnp.bfloat16)
    token_count = row_count * col_count
    flat = normed.reshape(frame_count * token_count, channels)
    query = (jnp.dot(flat, w_query, preferred_element_type=jnp.float32) + b_query).astype(
        jnp.bfloat16
    )
    folded = (
        jnp.dot(query, w_key.T, preferred_element_type=jnp.float32) * (1.0 / math.sqrt(channels))
    ).astype(jnp.bfloat16)
    folded = folded.reshape(frame_count, token_count, channels)

    keys = lax.all_gather(normed, "space", axis=1, tiled=True)
    keys = keys.reshape(frame_count, height * col_count, channels)
    scores = jnp.einsum("fqc,fkc->fqk", folded, keys, preferred_element_type=jnp.float32)
    top = jnp.max(scores, axis=-1, keepdims=True)
    weights = jnp.exp(scores - top)
    total = jnp.sum(weights, axis=-1, keepdims=True)
    accum = jnp.einsum(
        "fqk,fkc->fqc", weights.astype(jnp.bfloat16), keys, preferred_element_type=jnp.float32
    )
    mixed = (accum / total).astype(jnp.bfloat16).reshape(-1, channels)
    value = (jnp.dot(mixed, w_value, preferred_element_type=jnp.float32) + b_value).astype(
        jnp.bfloat16
    )
    decoded = (
        residual.reshape(-1, channels)
        + jnp.dot(value, w_out, preferred_element_type=jnp.float32)
        + b_out
    )
    return decoded.reshape(frame_count, 1, row_count, col_count, channels)


def solution(mesh):
    placed = (P("clips", "tm", "space", None, None),) + (P(),) * 14
    return jax.shard_map(
        local,
        mesh=mesh,
        in_specs=placed,
        out_specs=P("clips", "tm", "space", None, None),
        check_vma=False,
    )
```

```python
import math

import jax
import jax.numpy as jnp
from jax import lax
from jax.sharding import PartitionSpec as P

epsilon = 1e-06
HALO = 2


def rms_scale(values, gain):
    return values * lax.rsqrt(jnp.mean(values * values, axis=-1, keepdims=True) + epsilon) * gain


def conv_rows(source, taps):
    return lax.conv_general_dilated(
        source,
        taps,
        window_strides=(1, 1),
        padding=((0, 0), (1, 1)),
        dimension_numbers=("NHWC", "HWIO", "NHWC"),
        preferred_element_type=jnp.float32,
    )


def causal_time_conv(seq, weight):
    frame_total = seq.shape[0]
    out = None
    for p in range(3):
        lag = 2 - p
        if lag >= frame_total:
            continue
        part = conv_rows(seq[: frame_total - lag], weight[p])
        if lag:
            part = jnp.pad(part, ((lag, 0), (0, 0), (0, 0), (0, 0)))
        out = part if out is None else out + part
    return out


def local(
    frames,
    norm1_gain,
    conv1_weight,
    conv1_bias,
    norm2_gain,
    conv2_weight,
    conv2_bias,
    attn_gain,
    w_query,
    b_query,
    w_key,
    w_value,
    b_value,
    w_out,
    b_out,
):
    own = frames[:, 0]
    frame_count, row_count, col_count, channels = own.shape
    inner = lax.axis_size("inner")
    bands = lax.axis_size("outer") * inner
    band = lax.axis_index("outer") * inner + lax.axis_index("inner")
    is_first = lax.axis_index("tm") == 0
    height = bands * row_count

    partner = lax.ppermute(own, "tm", [(0, 1), (1, 0)])
    even = jnp.where(is_first, own, partner)
    odd = jnp.where(is_first, partner, own)
    seq = jnp.stack([even, odd], axis=1).reshape(2 * frame_count, row_count, col_count, channels)

    up = [(2 * i, 2 * i + 2) for i in range(bands - 1)]
    down = [(2 * i + 3, 2 * i + 1) for i in range(bands - 1)]
    edge = jnp.where(is_first, seq[:, row_count - HALO :], seq[:, :HALO])
    arrived = lax.ppermute(edge, ("outer", "inner", "tm"), up + down)
    swapped = lax.ppermute(arrived, "tm", [(0, 1), (1, 0)])
    above = jnp.where(is_first, arrived, swapped)
    below = jnp.where(is_first, swapped, arrived)
    ext = jnp.concatenate([above, seq, below], axis=1)

    first_act = jax.nn.silu(rms_scale(ext.astype(jnp.float32), norm1_gain)).astype(jnp.bfloat16)
    first_out = causal_time_conv(first_act, conv1_weight) + conv1_bias
    rows = band * row_count - 1 + lax.broadcasted_iota(jnp.int32, (1, row_count + 2, 1, 1), 1)
    inside = (rows >= 0) & (rows < height)
    second_act = jnp.where(
        inside, jax.nn.silu(rms_scale(first_out, norm2_gain)), 0.0
    ).astype(jnp.bfloat16)

    pairs = second_act.reshape(frame_count, 2, row_count + 2, col_count, channels)
    sa_even = pairs[:, 0]
    sa_odd = pairs[:, 1]
    zero = jnp.zeros_like(sa_even[:1])
    odd_before = jnp.concatenate([zero, sa_odd[:-1]], axis=0)
    even_before = jnp.concatenate([zero, sa_even[:-1]], axis=0)
    current = jnp.where(is_first, sa_even, sa_odd)
    previous = jnp.where(is_first, odd_before, sa_even)
    second_out = conv_rows(current, conv2_weight[2]) + conv_rows(previous, conv2_weight[1])
    if frame_count > 1:
        oldest = jnp.where(is_first, even_before, odd_before)
        second_out = second_out + conv_rows(oldest, conv2_weight[0])
    second_out = second_out + conv2_bias

    frame_values = own.astype(jnp.float32)
    residual = frame_values + second_out
    normed = rms_scale(residual, attn_gain).astype(jnp.bfloat16)
    token_count = row_count * col_count
    flat = normed.reshape(frame_count * token_count, channels)
    query = (jnp.dot(flat, w_query, preferred_element_type=jnp.float32) + b_query).astype(
        jnp.bfloat16
    )
    folded = (
        jnp.dot(query, w_key.T, preferred_element_type=jnp.float32) * (1.0 / math.sqrt(channels))
    ).astype(jnp.bfloat16)
    folded = folded.reshape(frame_count, token_count, channels)

    keys = lax.all_gather(normed, "outer", axis=1, tiled=True)
    keys = keys.reshape(frame_count, -1, 1, row_count, col_count, channels)
    keys = lax.all_gather(keys, "inner", axis=2, tiled=True)
    keys = keys.reshape(frame_count, height * col_count, channels)
    scores = jnp.einsum("fqc,fkc->fqk", folded, keys, preferred_element_type=jnp.float32)
    top = jnp.max(scores, axis=-1, keepdims=True)
    weights = jnp.exp(scores - top)
    total = jnp.sum(weights, axis=-1, keepdims=True)
    accum = jnp.einsum(
        "fqk,fkc->fqc", weights.astype(jnp.bfloat16), keys, preferred_element_type=jnp.float32
    )
    mixed = (accum / total).astype(jnp.bfloat16).reshape(-1, channels)
    value = (jnp.dot(mixed, w_value, preferred_element_type=jnp.float32) + b_value).astype(
        jnp.bfloat16
    )
    decoded = (
        residual.reshape(-1, channels)
        + jnp.dot(value, w_out, preferred_element_type=jnp.float32)
        + b_out
    )
    return decoded.reshape(frame_count, 1, row_count, col_count, channels)


def solution(mesh):
    clips, bands, cores = mesh.devices.shape
    split = jax.sharding.Mesh(
        mesh.devices.reshape(clips, bands // 2, 2, cores), ("clips", "outer", "inner", "tm")
    )
    banded = P("clips", "tm", ("outer", "inner"), None, None)
    placed = (banded,) + (P(),) * 14
    return jax.shard_map(
        local,
        mesh=split,
        in_specs=placed,
        out_specs=banded,
        check_vma=False,
    )
```

```python
import functools
import math

import jax
import jax.numpy as jnp
from jax import lax
from jax.experimental import pallas as pl
from jax.experimental.pallas import tpu as pltpu
from jax.sharding import PartitionSpec as P

epsilon = 1e-06
HALO = 2


def rms_scale(values, gain):
    return values * lax.rsqrt(jnp.mean(values * values, axis=-1, keepdims=True) + epsilon) * gain


def conv_rows(source, taps):
    return lax.conv_general_dilated(
        source,
        taps,
        window_strides=(1, 1),
        padding=((0, 0), (1, 1)),
        dimension_numbers=("NHWC", "HWIO", "NHWC"),
        preferred_element_type=jnp.float32,
    )


def causal_time_conv(seq, weight):
    frame_total = seq.shape[0]
    out = None
    for p in range(3):
        lag = 2 - p
        if lag >= frame_total:
            continue
        part = conv_rows(seq[: frame_total - lag], weight[p])
        if lag:
            part = jnp.pad(part, ((lag, 0), (0, 0), (0, 0), (0, 0)))
        out = part if out is None else out + part
    return out


def _rms(v, g):
    return v * lax.rsqrt(jnp.mean(v * v, axis=-1, keepdims=True) + epsilon) * g

def _silu(v):
    return v * (1.0 / (1.0 + jnp.exp(-v)))

def block_kernel(cols, frame_count, params, ext_ref, own_ref, g1_ref, w1_ref, b1_ref, g2_ref,
                 w2_ref, b2_ref, ga_ref, res_ref, normed_ref):
    total = 2 * frame_count
    p_in = ext_ref.shape[1]
    p_mid = p_in - 2 * cols
    p_out = p_mid - 2 * cols

    def shifted(a):
        n = a.shape[0]
        col = lax.broadcasted_iota(jnp.int32, (n, 1), 0) % cols
        left = jnp.where(col == 0, 0.0, pltpu.roll(a, 1, 0))
        right = jnp.where(col == cols - 1, 0.0, pltpu.roll(a, n - 1, 0))
        return [left.astype(jnp.bfloat16), a.astype(jnp.bfloat16), right.astype(jnp.bfloat16)]

    def conv_frame(sources, w_ref, out_rows):
        acc = None
        for p, trip in enumerate(sources):
            if trip is None:
                continue
            for q in range(3):
                for s in range(3):
                    window = trip[s][q * cols: q * cols + out_rows]
                    part = jnp.dot(window, w_ref[(p * 3 + q) * 3 + s], preferred_element_type=jnp.float32)
                    acc = part if acc is None else acc + part
        return acc

    g1 = g1_ref[...]
    act1 = [shifted(_silu(_rms(ext_ref[t].astype(jnp.float32), g1)).astype(jnp.bfloat16).astype(jnp.float32)) for t in range(total)]
    lo = params[0]
    hi = params[1]
    first = params[2] == 1
    row = lax.broadcasted_iota(jnp.int32, (p_mid, 1), 0) // cols
    inside = (row >= lo) & (row < hi)
    g2 = g2_ref[...]
    b1 = b1_ref[...]
    act2 = []
    for j in range(total):
        srcs = [act1[j + p - 2] if j + p - 2 >= 0 else None for p in range(3)]
        out1 = conv_frame(srcs, w1_ref, p_mid) + b1
        act2.append(jnp.where(inside, _silu(_rms(out1, g2)), 0.0).astype(jnp.bfloat16).astype(jnp.float32))
    b2 = b2_ref[...]
    ga = ga_ref[...]
    zero = None
    for k in range(frame_count):
        def pick(t_even):
            a = act2[t_even] if 0 <= t_even < total else None
            b = act2[t_even + 1] if 0 <= t_even + 1 < total else None
            if a is None and b is None:
                return None
            a = jnp.zeros_like(act2[0]) if a is None else a
            b = jnp.zeros_like(act2[0]) if b is None else b
            return shifted(jnp.where(first, a, b))
        srcs = [pick(2 * k - 2), pick(2 * k - 1), pick(2 * k)]
        out2 = conv_frame(srcs, w2_ref, p_out) + b2
        res = own_ref[k].astype(jnp.float32) + out2
        res_ref[k] = res
        normed_ref[k] = _rms(res, ga).astype(jnp.bfloat16)

def resnet_block(ext, own, params, g1, w1, b1, g2, w2, b2, ga, cols):
    total, p_in, c = ext.shape
    frame_count, p_out, _ = own.shape
    vm = pl.BlockSpec(memory_space=pltpu.VMEM)
    sm = pl.BlockSpec(memory_space=pltpu.SMEM)
    return pl.pallas_call(
        functools.partial(block_kernel, cols, frame_count),
        out_shape=(jax.ShapeDtypeStruct((frame_count, p_out, c), jnp.float32),
                   jax.ShapeDtypeStruct((frame_count, p_out, c), jnp.bfloat16)),
        in_specs=[sm] + [vm] * 9,
        out_specs=(vm, vm),
    )(params, ext, own, g1.reshape(1, c), w1.reshape(27, c, c), b1.reshape(1, c), g2.reshape(1, c),
      w2.reshape(27, c, c), b2.reshape(1, c), ga.reshape(1, c))


def local(
    frames,
    norm1_gain,
    conv1_weight,
    conv1_bias,
    norm2_gain,
    conv2_weight,
    conv2_bias,
    attn_gain,
    w_query,
    b_query,
    w_key,
    w_value,
    b_value,
    w_out,
    b_out,
):
    own = frames[:, 0]
    frame_count, row_count, col_count, channels = own.shape
    inner = lax.axis_size("inner")
    bands = lax.axis_size("outer") * inner
    band = lax.axis_index("outer") * inner + lax.axis_index("inner")
    is_first = lax.axis_index("tm") == 0
    height = bands * row_count

    partner = lax.ppermute(own, "tm", [(0, 1), (1, 0)])
    even = jnp.where(is_first, own, partner)
    odd = jnp.where(is_first, partner, own)
    seq = jnp.stack([even, odd], axis=1).reshape(2 * frame_count, row_count, col_count, channels)

    up = [(2 * i, 2 * i + 2) for i in range(bands - 1)]
    down = [(2 * i + 3, 2 * i + 1) for i in range(bands - 1)]
    edge = jnp.where(is_first, seq[:, row_count - HALO :], seq[:, :HALO])
    arrived = lax.ppermute(edge, ("outer", "inner", "tm"), up + down)
    swapped = lax.ppermute(arrived, "tm", [(0, 1), (1, 0)])
    above = jnp.where(is_first, arrived, swapped)
    below = jnp.where(is_first, swapped, arrived)
    ext = jnp.concatenate([above, seq, below], axis=1)

    token_count = row_count * col_count
    params = jnp.stack(
        [1 - band * row_count, height - band * row_count + 1, is_first.astype(jnp.int32)]
    ).astype(jnp.int32)
    residual, normed = resnet_block(
        ext.reshape(2 * frame_count, -1, channels),
        own.reshape(frame_count, token_count, channels),
        params,
        norm1_gain,
        conv1_weight,
        conv1_bias,
        norm2_gain,
        conv2_weight,
        conv2_bias,
        attn_gain,
        col_count,
    )
    normed = normed.reshape(frame_count, row_count, col_count, channels)
    flat = normed.reshape(frame_count * token_count, channels)
    query = (jnp.dot(flat, w_query, preferred_element_type=jnp.float32) + b_query).astype(
        jnp.bfloat16
    )
    folded = (
        jnp.dot(query, w_key.T, preferred_element_type=jnp.float32) * (1.0 / math.sqrt(channels))
    ).astype(jnp.bfloat16)
    folded = folded.reshape(frame_count, token_count, channels)

    keys = lax.all_gather(normed, "outer", axis=1, tiled=True)
    keys = keys.reshape(frame_count, -1, 1, row_count, col_count, channels)
    keys = lax.all_gather(keys, "inner", axis=2, tiled=True)
    keys = keys.reshape(frame_count, height * col_count, channels)
    scores = jnp.einsum("fqc,fkc->fqk", folded, keys, preferred_element_type=jnp.float32)
    top = jnp.max(scores, axis=-1, keepdims=True)
    weights = jnp.exp(scores - top)
    total = jnp.sum(weights, axis=-1, keepdims=True)
    accum = jnp.einsum(
        "fqk,fkc->fqc", weights.astype(jnp.bfloat16), keys, preferred_element_type=jnp.float32
    )
    mixed = (accum / total).astype(jnp.bfloat16).reshape(-1, channels)
    value = (jnp.dot(mixed, w_value, preferred_element_type=jnp.float32) + b_value).astype(
        jnp.bfloat16
    )
    decoded = (
        residual.reshape(-1, channels)
        + jnp.dot(value, w_out, preferred_element_type=jnp.float32)
        + b_out
    )
    return decoded.reshape(frame_count, 1, row_count, col_count, channels)


def solution(mesh):
    clips, bands, cores = mesh.devices.shape
    split = jax.sharding.Mesh(
        mesh.devices.reshape(clips, bands // 2, 2, cores), ("clips", "outer", "inner", "tm")
    )
    banded = P("clips", "tm", ("outer", "inner"), None, None)
    placed = (banded,) + (P(),) * 14
    return jax.shard_map(
        local,
        mesh=split,
        in_specs=placed,
        out_specs=banded,
        check_vma=False,
    )
```

```python
import functools
import math

import jax
import jax.numpy as jnp
from jax import lax
from jax.experimental import pallas as pl
from jax.experimental.pallas import tpu as pltpu
from jax.sharding import PartitionSpec as P

epsilon = 1e-06
HALO = 2


def rms_scale(values, gain):
    return values * lax.rsqrt(jnp.mean(values * values, axis=-1, keepdims=True) + epsilon) * gain


def conv_rows(source, taps):
    return lax.conv_general_dilated(
        source,
        taps,
        window_strides=(1, 1),
        padding=((0, 0), (1, 1)),
        dimension_numbers=("NHWC", "HWIO", "NHWC"),
        preferred_element_type=jnp.float32,
    )


def causal_time_conv(seq, weight):
    frame_total = seq.shape[0]
    out = None
    for p in range(3):
        lag = 2 - p
        if lag >= frame_total:
            continue
        part = conv_rows(seq[: frame_total - lag], weight[p])
        if lag:
            part = jnp.pad(part, ((lag, 0), (0, 0), (0, 0), (0, 0)))
        out = part if out is None else out + part
    return out


def _rms(v, g):
    return v * lax.rsqrt(jnp.mean(v * v, axis=-1, keepdims=True) + epsilon) * g

def _silu(v):
    return v * (1.0 / (1.0 + jnp.exp(-v)))

def block_kernel(cols, frame_count, params, ext_ref, own_ref, g1_ref, w1_ref, b1_ref, g2_ref,
                 w2_ref, b2_ref, ga_ref, res_ref, normed_ref):
    total = 2 * frame_count
    p_in = ext_ref.shape[1]
    p_mid = p_in - 2 * cols
    p_out = p_mid - 2 * cols

    def shifted(a):
        n = a.shape[0]
        col = lax.broadcasted_iota(jnp.int32, (n, 1), 0) % cols
        left = jnp.where(col == 0, 0.0, pltpu.roll(a, 1, 0))
        right = jnp.where(col == cols - 1, 0.0, pltpu.roll(a, n - 1, 0))
        return [left.astype(jnp.bfloat16), a.astype(jnp.bfloat16), right.astype(jnp.bfloat16)]

    def conv_frame(sources, w_ref, out_rows):
        acc = None
        for p, trip in enumerate(sources):
            if trip is None:
                continue
            for q in range(3):
                for s in range(3):
                    window = trip[s][q * cols: q * cols + out_rows]
                    part = jnp.dot(window, w_ref[(p * 3 + q) * 3 + s], preferred_element_type=jnp.float32)
                    acc = part if acc is None else acc + part
        return acc

    g1 = g1_ref[...]
    act1 = [shifted(_silu(_rms(ext_ref[t].astype(jnp.float32), g1)).astype(jnp.bfloat16).astype(jnp.float32)) for t in range(total)]
    lo = params[0]
    hi = params[1]
    first = params[2] == 1
    row = lax.broadcasted_iota(jnp.int32, (p_mid, 1), 0) // cols
    inside = (row >= lo) & (row < hi)
    g2 = g2_ref[...]
    b1 = b1_ref[...]
    act2 = []
    for j in range(total):
        srcs = [act1[j + p - 2] if j + p - 2 >= 0 else None for p in range(3)]
        out1 = conv_frame(srcs, w1_ref, p_mid) + b1
        act2.append(jnp.where(inside, _silu(_rms(out1, g2)), 0.0).astype(jnp.bfloat16).astype(jnp.float32))
    b2 = b2_ref[...]
    ga = ga_ref[...]
    zero = None
    for k in range(frame_count):
        def pick(t_even):
            a = act2[t_even] if 0 <= t_even < total else None
            b = act2[t_even + 1] if 0 <= t_even + 1 < total else None
            if a is None and b is None:
                return None
            a = jnp.zeros_like(act2[0]) if a is None else a
            b = jnp.zeros_like(act2[0]) if b is None else b
            return shifted(jnp.where(first, a, b))
        srcs = [pick(2 * k - 2), pick(2 * k - 1), pick(2 * k)]
        out2 = conv_frame(srcs, w2_ref, p_out) + b2
        res = own_ref[k].astype(jnp.float32) + out2
        res_ref[k] = res
        normed_ref[k] = _rms(res, ga).astype(jnp.bfloat16)

def resnet_block(ext, own, params, g1, w1, b1, g2, w2, b2, ga, cols):
    total, p_in, c = ext.shape
    frame_count, p_out, _ = own.shape
    vm = pl.BlockSpec(memory_space=pltpu.VMEM)
    sm = pl.BlockSpec(memory_space=pltpu.SMEM)
    return pl.pallas_call(
        functools.partial(block_kernel, cols, frame_count),
        out_shape=(jax.ShapeDtypeStruct((frame_count, p_out, c), jnp.float32),
                   jax.ShapeDtypeStruct((frame_count, p_out, c), jnp.bfloat16)),
        in_specs=[sm] + [vm] * 9,
        out_specs=(vm, vm),
    )(params, ext, own, g1.reshape(1, c), w1.reshape(27, c, c), b1.reshape(1, c), g2.reshape(1, c),
      w2.reshape(27, c, c), b2.reshape(1, c), ga.reshape(1, c))


def local(
    frames,
    norm1_gain,
    conv1_weight,
    conv1_bias,
    norm2_gain,
    conv2_weight,
    conv2_bias,
    attn_gain,
    w_query,
    b_query,
    w_key,
    w_value,
    b_value,
    w_out,
    b_out,
):
    own = frames[:, 0]
    frame_count, row_count, col_count, channels = own.shape
    inner = lax.axis_size("inner")
    bands = lax.axis_size("outer") * inner
    band = lax.axis_index("outer") * inner + lax.axis_index("inner")
    is_first = lax.axis_index("tm") == 0
    height = bands * row_count

    partner = lax.ppermute(own, "tm", [(0, 1), (1, 0)])
    even = jnp.where(is_first, own, partner)
    odd = jnp.where(is_first, partner, own)
    seq = jnp.stack([even, odd], axis=1).reshape(2 * frame_count, row_count, col_count, channels)

    up = [(2 * i, 2 * i + 2) for i in range(bands - 1)]
    down = [(2 * i + 3, 2 * i + 1) for i in range(bands - 1)]
    edge = jnp.where(is_first, seq[:, row_count - HALO :], seq[:, :HALO])
    arrived = lax.ppermute(edge, ("outer", "inner", "tm"), up + down)
    swapped = lax.ppermute(arrived, "tm", [(0, 1), (1, 0)])
    above = jnp.where(is_first, arrived, swapped)
    below = jnp.where(is_first, swapped, arrived)
    ext = jnp.concatenate([above, seq, below], axis=1)

    token_count = row_count * col_count
    params = jnp.stack(
        [1 - band * row_count, height - band * row_count + 1, is_first.astype(jnp.int32)]
    ).astype(jnp.int32)
    residual, normed = resnet_block(
        ext.reshape(2 * frame_count, -1, channels),
        own.reshape(frame_count, token_count, channels),
        params,
        norm1_gain,
        conv1_weight,
        conv1_bias,
        norm2_gain,
        conv2_weight,
        conv2_bias,
        attn_gain,
        col_count,
    )
    normed = normed.reshape(frame_count, row_count, col_count, channels)
    flat = normed.reshape(frame_count * token_count, channels)
    query = (jnp.dot(flat, w_query, preferred_element_type=jnp.float32) + b_query).astype(
        jnp.bfloat16
    )
    folded = (
        jnp.dot(query, w_key.T, preferred_element_type=jnp.float32) * (1.0 / math.sqrt(channels))
    ).astype(jnp.bfloat16)
    folded = folded.reshape(frame_count, token_count, channels)

    swap = [(0, 1), (1, 0)]
    partner_queries = lax.ppermute(folded, "inner", swap)
    keys = lax.all_gather(normed, "outer", axis=1, tiled=True)
    keys = keys.reshape(frame_count, -1, channels)
    queries = jnp.concatenate([folded, partner_queries], axis=1)
    scores = jnp.einsum("fqc,fkc->fqk", queries, keys, preferred_element_type=jnp.float32)
    top = jnp.max(scores, axis=-1, keepdims=True)
    weights = jnp.exp(scores - top)
    total = jnp.sum(weights, axis=-1, keepdims=True)
    accum = jnp.einsum(
        "fqk,fkc->fqc", weights.astype(jnp.bfloat16), keys, preferred_element_type=jnp.float32
    )
    packed = jnp.concatenate([accum, top, total], axis=-1)
    returned = lax.ppermute(packed[:, token_count:], "inner", swap)
    mine = packed[:, :token_count]
    top_mine = mine[..., channels : channels + 1]
    top_back = returned[..., channels : channels + 1]
    highest = jnp.maximum(top_mine, top_back)
    scale_mine = jnp.exp(top_mine - highest)
    scale_back = jnp.exp(top_back - highest)
    total = mine[..., channels + 1 :] * scale_mine + returned[..., channels + 1 :] * scale_back
    accum = mine[..., :channels] * scale_mine + returned[..., :channels] * scale_back
    mixed = (accum / total).astype(jnp.bfloat16).reshape(-1, channels)
    value = (jnp.dot(mixed, w_value, preferred_element_type=jnp.float32) + b_value).astype(
        jnp.bfloat16
    )
    decoded = (
        residual.reshape(-1, channels)
        + jnp.dot(value, w_out, preferred_element_type=jnp.float32)
        + b_out
    )
    return decoded.reshape(frame_count, 1, row_count, col_count, channels)


def solution(mesh):
    clips, bands, cores = mesh.devices.shape
    split = jax.sharding.Mesh(
        mesh.devices.reshape(clips, bands // 2, 2, cores), ("clips", "outer", "inner", "tm")
    )
    banded = P("clips", "tm", ("outer", "inner"), None, None)
    placed = (banded,) + (P(),) * 14
    return jax.shard_map(
        local,
        mesh=split,
        in_specs=placed,
        out_specs=banded,
        check_vma=False,
    )
```

```python
import functools
import math

import jax
import jax.numpy as jnp
from jax import lax
from jax.experimental import pallas as pl
from jax.experimental.pallas import tpu as pltpu
from jax.sharding import PartitionSpec as P

epsilon = 1e-06
HALO = 2


def rms_scale(values, gain):
    return values * lax.rsqrt(jnp.mean(values * values, axis=-1, keepdims=True) + epsilon) * gain


def conv_rows(source, taps):
    return lax.conv_general_dilated(
        source,
        taps,
        window_strides=(1, 1),
        padding=((0, 0), (1, 1)),
        dimension_numbers=("NHWC", "HWIO", "NHWC"),
        preferred_element_type=jnp.float32,
    )


def causal_time_conv(seq, weight):
    frame_total = seq.shape[0]
    out = None
    for p in range(3):
        lag = 2 - p
        if lag >= frame_total:
            continue
        part = conv_rows(seq[: frame_total - lag], weight[p])
        if lag:
            part = jnp.pad(part, ((lag, 0), (0, 0), (0, 0), (0, 0)))
        out = part if out is None else out + part
    return out


def _rms(v, g):
    return v * lax.rsqrt(jnp.mean(v * v, axis=-1, keepdims=True) + epsilon) * g

def _silu(v):
    return v * (1.0 / (1.0 + jnp.exp(-v)))

def block_kernel(cols, frame_count, ext_ref, g1_ref, w1_ref, b1_ref, g2_ref,
                 w2_ref, b2_ref, ga_ref, res_ref, normed_ref):
    total = 2 * frame_count
    p_in = ext_ref.shape[1]
    p_mid = p_in - 2 * cols
    p_out = p_mid - 2 * cols

    def shifted(a):
        n = a.shape[0]
        col = lax.broadcasted_iota(jnp.int32, (n, 1), 0) % cols
        left = jnp.where(col == 0, 0.0, pltpu.roll(a, 1, 0))
        right = jnp.where(col == cols - 1, 0.0, pltpu.roll(a, n - 1, 0))
        return [left.astype(jnp.bfloat16), a.astype(jnp.bfloat16), right.astype(jnp.bfloat16)]

    def conv_frame(sources, w_ref, out_rows):
        acc = None
        for p, trip in enumerate(sources):
            if trip is None:
                continue
            for q in range(3):
                for s in range(3):
                    window = trip[s][q * cols: q * cols + out_rows]
                    part = jnp.dot(window, w_ref[(p * 3 + q) * 3 + s], preferred_element_type=jnp.float32)
                    acc = part if acc is None else acc + part
        return acc

    g1 = g1_ref[...]
    act1 = [shifted(_silu(_rms(ext_ref[t].astype(jnp.float32), g1)).astype(jnp.bfloat16).astype(jnp.float32)) for t in range(total)]
    inner = lax.axis_size("inner")
    band = lax.axis_index("outer") * inner + lax.axis_index("inner")
    band_rows = p_out // cols
    height = lax.axis_size("outer") * inner * band_rows
    lo = 1 - band * band_rows
    hi = height - band * band_rows + 1
    first = lax.axis_index("tm") == 0
    row = lax.broadcasted_iota(jnp.int32, (p_mid, 1), 0) // cols
    inside = (row >= lo) & (row < hi)
    g2 = g2_ref[...]
    b1 = b1_ref[...]
    act2 = []
    for j in range(total):
        srcs = [act1[j + p - 2] if j + p - 2 >= 0 else None for p in range(3)]
        out1 = conv_frame(srcs, w1_ref, p_mid) + b1
        act2.append(jnp.where(inside, _silu(_rms(out1, g2)), 0.0).astype(jnp.bfloat16).astype(jnp.float32))
    b2 = b2_ref[...]
    ga = ga_ref[...]
    zero = None
    for k in range(frame_count):
        def pick(t_even):
            a = act2[t_even] if 0 <= t_even < total else None
            b = act2[t_even + 1] if 0 <= t_even + 1 < total else None
            if a is None and b is None:
                return None
            a = jnp.zeros_like(act2[0]) if a is None else a
            b = jnp.zeros_like(act2[0]) if b is None else b
            return shifted(jnp.where(first, a, b))
        srcs = [pick(2 * k - 2), pick(2 * k - 1), pick(2 * k)]
        out2 = conv_frame(srcs, w2_ref, p_out) + b2
        body = slice(HALO * cols, HALO * cols + p_out)
        own = jnp.where(first, ext_ref[2 * k, body], ext_ref[2 * k + 1, body])
        res = own.astype(jnp.float32) + out2
        res_ref[k] = res
        normed_ref[k] = _rms(res, ga).astype(jnp.bfloat16)

def resnet_block(ext, g1, w1, b1, g2, w2, b2, ga, cols):
    total, p_in, c = ext.shape
    frame_count = total // 2
    p_out = p_in - 4 * cols
    vm = pl.BlockSpec(memory_space=pltpu.VMEM)
    return pl.pallas_call(
        functools.partial(block_kernel, cols, frame_count),
        out_shape=(jax.ShapeDtypeStruct((frame_count, p_out, c), jnp.float32),
                   jax.ShapeDtypeStruct((frame_count, p_out, c), jnp.bfloat16)),
        in_specs=[vm] * 8,
        out_specs=(vm, vm),
    )(ext, g1.reshape(1, c), w1.reshape(27, c, c), b1.reshape(1, c), g2.reshape(1, c),
      w2.reshape(27, c, c), b2.reshape(1, c), ga.reshape(1, c))


def local(
    frames,
    norm1_gain,
    conv1_weight,
    conv1_bias,
    norm2_gain,
    conv2_weight,
    conv2_bias,
    attn_gain,
    w_query,
    b_query,
    w_key,
    w_value,
    b_value,
    w_out,
    b_out,
):
    own = frames[:, 0]
    frame_count, row_count, col_count, channels = own.shape
    inner = lax.axis_size("inner")
    bands = lax.axis_size("outer") * inner
    band = lax.axis_index("outer") * inner + lax.axis_index("inner")
    is_first = lax.axis_index("tm") == 0
    height = bands * row_count

    partner = lax.ppermute(own, "tm", [(0, 1), (1, 0)])
    even = jnp.where(is_first, own, partner)
    odd = jnp.where(is_first, partner, own)
    seq = jnp.stack([even, odd], axis=1).reshape(2 * frame_count, row_count, col_count, channels)

    up = [(2 * i, 2 * i + 2) for i in range(bands - 1)]
    down = [(2 * i + 3, 2 * i + 1) for i in range(bands - 1)]
    edge = jnp.where(is_first, seq[:, row_count - HALO :], seq[:, :HALO])
    arrived = lax.ppermute(edge, ("outer", "inner", "tm"), up + down)
    swapped = lax.ppermute(arrived, "tm", [(0, 1), (1, 0)])
    above = jnp.where(is_first, arrived, swapped)
    below = jnp.where(is_first, swapped, arrived)
    ext = jnp.concatenate([above, seq, below], axis=1)

    token_count = row_count * col_count
    residual, normed = resnet_block(
        ext.reshape(2 * frame_count, -1, channels),
        norm1_gain,
        conv1_weight,
        conv1_bias,
        norm2_gain,
        conv2_weight,
        conv2_bias,
        attn_gain,
        col_count,
    )
    normed = normed.reshape(frame_count, row_count, col_count, channels)
    flat = normed.reshape(frame_count * token_count, channels)
    query = (jnp.dot(flat, w_query, preferred_element_type=jnp.float32) + b_query).astype(
        jnp.bfloat16
    )
    folded = (
        jnp.dot(query, w_key.T, preferred_element_type=jnp.float32) * (1.0 / math.sqrt(channels))
    ).astype(jnp.bfloat16)
    folded = folded.reshape(frame_count, token_count, channels)

    swap = [(0, 1), (1, 0)]
    partner_queries = lax.ppermute(folded, "inner", swap)
    keys = lax.all_gather(normed, "outer", axis=1, tiled=True)
    keys = keys.reshape(frame_count, -1, channels)
    def partial(queries):
        scores = jnp.einsum("fqc,fkc->fqk", queries, keys, preferred_element_type=jnp.float32)
        top = jnp.max(scores, axis=-1, keepdims=True)
        weights = jnp.exp(scores - top)
        total = jnp.sum(weights, axis=-1, keepdims=True)
        accum = jnp.einsum(
            "fqk,fkc->fqc", weights.astype(jnp.bfloat16), keys, preferred_element_type=jnp.float32
        )
        return jnp.concatenate([accum, top, total], axis=-1)

    returned = lax.ppermute(partial(partner_queries), "inner", swap)
    mine = partial(folded)
    top_mine = mine[..., channels : channels + 1]
    top_back = returned[..., channels : channels + 1]
    highest = jnp.maximum(top_mine, top_back)
    scale_mine = jnp.exp(top_mine - highest)
    scale_back = jnp.exp(top_back - highest)
    total = mine[..., channels + 1 :] * scale_mine + returned[..., channels + 1 :] * scale_back
    accum = mine[..., :channels] * scale_mine + returned[..., :channels] * scale_back
    mixed = (accum / total).astype(jnp.bfloat16).reshape(-1, channels)
    value = (jnp.dot(mixed, w_value, preferred_element_type=jnp.float32) + b_value).astype(
        jnp.bfloat16
    )
    decoded = (
        residual.reshape(-1, channels)
        + jnp.dot(value, w_out, preferred_element_type=jnp.float32)
        + b_out
    )
    return decoded.reshape(frame_count, 1, row_count, col_count, channels)


def solution(mesh):
    clips, bands, cores = mesh.devices.shape
    split = jax.sharding.Mesh(
        mesh.devices.reshape(clips, bands // 2, 2, cores), ("clips", "outer", "inner", "tm")
    )
    banded = P("clips", "tm", ("outer", "inner"), None, None)
    placed = (banded,) + (P(),) * 14
    return jax.shard_map(
        local,
        mesh=split,
        in_specs=placed,
        out_specs=banded,
        check_vma=False,
    )
```

```python
import functools
import math

import jax
import jax.numpy as jnp
from jax import lax
from jax.experimental import pallas as pl
from jax.experimental.pallas import tpu as pltpu
from jax.sharding import PartitionSpec as P

epsilon = 1e-06
HALO = 2


def rms_scale(values, gain):
    return values * lax.rsqrt(jnp.mean(values * values, axis=-1, keepdims=True) + epsilon) * gain


def conv_rows(source, taps):
    return lax.conv_general_dilated(
        source,
        taps,
        window_strides=(1, 1),
        padding=((0, 0), (1, 1)),
        dimension_numbers=("NHWC", "HWIO", "NHWC"),
        preferred_element_type=jnp.float32,
    )


def causal_time_conv(seq, weight):
    frame_total = seq.shape[0]
    out = None
    for p in range(3):
        lag = 2 - p
        if lag >= frame_total:
            continue
        part = conv_rows(seq[: frame_total - lag], weight[p])
        if lag:
            part = jnp.pad(part, ((lag, 0), (0, 0), (0, 0), (0, 0)))
        out = part if out is None else out + part
    return out


def _rms(v, g):
    return v * lax.rsqrt(jnp.mean(v * v, axis=-1, keepdims=True) + epsilon) * g

def _silu(v):
    return v * (1.0 / (1.0 + jnp.exp(-v)))

def taps_used(total, frame_count):
    first_conv = [p for p in range(3) if total - 1 + p - 2 >= 0]
    second_conv = [p for p in range(3) if 2 * frame_count - 1 + p - 2 >= 0]
    return first_conv, second_conv


def block_kernel(cols, frame_count, ext_ref, g1_ref, w1_hbm, b1_ref, g2_ref,
                 w2_hbm, b2_ref, ga_ref, res_ref, normed_ref, w1_ref, w2_ref, sems):
    total = 2 * frame_count
    used1, used2 = taps_used(total, frame_count)
    pending = {}
    for slot, (hbm, buf, used) in enumerate(((w1_hbm, w1_ref, used1), (w2_hbm, w2_ref, used2))):
        for p in used:
            chunk = pl.ds(p * 9, 9)
            copy = pltpu.make_async_copy(hbm.at[chunk], buf.at[chunk], sems.at[slot * 3 + p])
            copy.start()
            pending[(slot, p)] = copy

    def ready(slot, p):
        copy = pending.pop((slot, p), None)
        if copy is not None:
            copy.wait()
    p_in = ext_ref.shape[1]
    p_mid = p_in - 2 * cols
    p_out = p_mid - 2 * cols

    def shifted(a):
        n = a.shape[0]
        col = lax.broadcasted_iota(jnp.int32, (n, 1), 0) % cols
        left = jnp.where(col == 0, 0.0, pltpu.roll(a, 1, 0))
        right = jnp.where(col == cols - 1, 0.0, pltpu.roll(a, n - 1, 0))
        return [left.astype(jnp.bfloat16), a.astype(jnp.bfloat16), right.astype(jnp.bfloat16)]

    def conv_frame(sources, w_ref, out_rows):
        acc = None
        for p, trip in enumerate(sources):
            if trip is None:
                continue
            ready(0 if w_ref is w1_ref else 1, p)
            for q in range(3):
                for s in range(3):
                    window = trip[s][q * cols: q * cols + out_rows]
                    part = jnp.dot(window, w_ref[(p * 3 + q) * 3 + s], preferred_element_type=jnp.float32)
                    acc = part if acc is None else acc + part
        return acc

    g1 = g1_ref[...]
    act1 = [shifted(_silu(_rms(ext_ref[t].astype(jnp.float32), g1)).astype(jnp.bfloat16).astype(jnp.float32)) for t in range(total)]
    inner = lax.axis_size("inner")
    band = lax.axis_index("outer") * inner + lax.axis_index("inner")
    band_rows = p_out // cols
    height = lax.axis_size("outer") * inner * band_rows
    lo = 1 - band * band_rows
    hi = height - band * band_rows + 1
    first = lax.axis_index("tm") == 0
    row = lax.broadcasted_iota(jnp.int32, (p_mid, 1), 0) // cols
    inside = (row >= lo) & (row < hi)
    g2 = g2_ref[...]
    b1 = b1_ref[...]
    act2 = []
    for j in range(total):
        srcs = [act1[j + p - 2] if j + p - 2 >= 0 else None for p in range(3)]
        out1 = conv_frame(srcs, w1_ref, p_mid) + b1
        act2.append(jnp.where(inside, _silu(_rms(out1, g2)), 0.0).astype(jnp.bfloat16).astype(jnp.float32))
    b2 = b2_ref[...]
    ga = ga_ref[...]
    zero = None
    for k in range(frame_count):
        def pick(t_even):
            a = act2[t_even] if 0 <= t_even < total else None
            b = act2[t_even + 1] if 0 <= t_even + 1 < total else None
            if a is None and b is None:
                return None
            a = jnp.zeros_like(act2[0]) if a is None else a
            b = jnp.zeros_like(act2[0]) if b is None else b
            return shifted(jnp.where(first, a, b))
        srcs = [pick(2 * k - 2), pick(2 * k - 1), pick(2 * k)]
        out2 = conv_frame(srcs, w2_ref, p_out) + b2
        body = slice(HALO * cols, HALO * cols + p_out)
        own = jnp.where(first, ext_ref[2 * k, body], ext_ref[2 * k + 1, body])
        res = own.astype(jnp.float32) + out2
        res_ref[k] = res
        normed_ref[k] = _rms(res, ga).astype(jnp.bfloat16)

def resnet_block(ext, g1, w1, b1, g2, w2, b2, ga, cols):
    total, p_in, c = ext.shape
    frame_count = total // 2
    p_out = p_in - 4 * cols
    vm = pl.BlockSpec(memory_space=pltpu.VMEM)
    hbm = pl.BlockSpec(memory_space=pl.ANY)
    return pl.pallas_call(
        functools.partial(block_kernel, cols, frame_count),
        out_shape=(jax.ShapeDtypeStruct((frame_count, p_out, c), jnp.float32),
                   jax.ShapeDtypeStruct((frame_count, p_out, c), jnp.bfloat16)),
        in_specs=[vm, vm, hbm, vm, vm, hbm, vm, vm],
        out_specs=(vm, vm),
        scratch_shapes=[
            pltpu.VMEM((27, c, c), jnp.bfloat16),
            pltpu.VMEM((27, c, c), jnp.bfloat16),
            pltpu.SemaphoreType.DMA((6,)),
        ],
    )(ext, g1.reshape(1, c), w1.reshape(27, c, c), b1.reshape(1, c), g2.reshape(1, c),
      w2.reshape(27, c, c), b2.reshape(1, c), ga.reshape(1, c))


def local(
    frames,
    norm1_gain,
    conv1_weight,
    conv1_bias,
    norm2_gain,
    conv2_weight,
    conv2_bias,
    attn_gain,
    w_query,
    b_query,
    w_key,
    w_value,
    b_value,
    w_out,
    b_out,
):
    own = frames[:, 0]
    frame_count, row_count, col_count, channels = own.shape
    inner = lax.axis_size("inner")
    bands = lax.axis_size("outer") * inner
    band = lax.axis_index("outer") * inner + lax.axis_index("inner")
    is_first = lax.axis_index("tm") == 0
    height = bands * row_count

    partner = lax.ppermute(own, "tm", [(0, 1), (1, 0)])
    even = jnp.where(is_first, own, partner)
    odd = jnp.where(is_first, partner, own)
    seq = jnp.stack([even, odd], axis=1).reshape(2 * frame_count, row_count, col_count, channels)

    up = [(2 * i, 2 * i + 2) for i in range(bands - 1)]
    down = [(2 * i + 3, 2 * i + 1) for i in range(bands - 1)]
    edge = jnp.where(is_first, seq[:, row_count - HALO :], seq[:, :HALO])
    arrived = lax.ppermute(edge, ("outer", "inner", "tm"), up + down)
    swapped = lax.ppermute(arrived, "tm", [(0, 1), (1, 0)])
    above = jnp.where(is_first, arrived, swapped)
    below = jnp.where(is_first, swapped, arrived)
    ext = jnp.concatenate([above, seq, below], axis=1)

    token_count = row_count * col_count
    residual, normed = resnet_block(
        ext.reshape(2 * frame_count, -1, channels),
        norm1_gain,
        conv1_weight,
        conv1_bias,
        norm2_gain,
        conv2_weight,
        conv2_bias,
        attn_gain,
        col_count,
    )
    normed = normed.reshape(frame_count, row_count, col_count, channels)
    flat = normed.reshape(frame_count * token_count, channels)
    query = (jnp.dot(flat, w_query, preferred_element_type=jnp.float32) + b_query).astype(
        jnp.bfloat16
    )
    folded = (
        jnp.dot(query, w_key.T, preferred_element_type=jnp.float32) * (1.0 / math.sqrt(channels))
    ).astype(jnp.bfloat16)
    folded = folded.reshape(frame_count, token_count, channels)

    swap = [(0, 1), (1, 0)]
    partner_queries = lax.ppermute(folded, "inner", swap)
    keys = lax.all_gather(normed, "outer", axis=1, tiled=True)
    keys = keys.reshape(frame_count, -1, channels)
    def partial(queries):
        scores = jnp.einsum("fqc,fkc->fqk", queries, keys, preferred_element_type=jnp.float32)
        top = jnp.max(scores, axis=-1, keepdims=True)
        weights = jnp.exp(scores - top)
        total = jnp.sum(weights, axis=-1, keepdims=True)
        accum = jnp.einsum(
            "fqk,fkc->fqc", weights.astype(jnp.bfloat16), keys, preferred_element_type=jnp.float32
        )
        return jnp.concatenate([accum, top, total], axis=-1)

    returned = lax.ppermute(partial(partner_queries), "inner", swap)
    mine = partial(folded)
    top_mine = mine[..., channels : channels + 1]
    top_back = returned[..., channels : channels + 1]
    highest = jnp.maximum(top_mine, top_back)
    scale_mine = jnp.exp(top_mine - highest)
    scale_back = jnp.exp(top_back - highest)
    total = mine[..., channels + 1 :] * scale_mine + returned[..., channels + 1 :] * scale_back
    accum = mine[..., :channels] * scale_mine + returned[..., :channels] * scale_back
    mixed = (accum / total).astype(jnp.bfloat16).reshape(-1, channels)
    value = (jnp.dot(mixed, w_value, preferred_element_type=jnp.float32) + b_value).astype(
        jnp.bfloat16
    )
    decoded = (
        residual.reshape(-1, channels)
        + jnp.dot(value, w_out, preferred_element_type=jnp.float32)
        + b_out
    )
    return decoded.reshape(frame_count, 1, row_count, col_count, channels)


def solution(mesh):
    clips, bands, cores = mesh.devices.shape
    split = jax.sharding.Mesh(
        mesh.devices.reshape(clips, bands // 2, 2, cores), ("clips", "outer", "inner", "tm")
    )
    banded = P("clips", "tm", ("outer", "inner"), None, None)
    placed = (banded,) + (P(),) * 14
    return jax.shard_map(
        local,
        mesh=split,
        in_specs=placed,
        out_specs=banded,
        check_vma=False,
    )
```

```python
import functools
import math

import jax
import jax.numpy as jnp
from jax import lax
from jax.experimental import pallas as pl
from jax.experimental.pallas import tpu as pltpu
from jax.sharding import PartitionSpec as P

epsilon = 1e-06
HALO = 2


def rms_scale(values, gain):
    return values * lax.rsqrt(jnp.mean(values * values, axis=-1, keepdims=True) + epsilon) * gain


def conv_rows(source, taps):
    return lax.conv_general_dilated(
        source,
        taps,
        window_strides=(1, 1),
        padding=((0, 0), (1, 1)),
        dimension_numbers=("NHWC", "HWIO", "NHWC"),
        preferred_element_type=jnp.float32,
    )


def causal_time_conv(seq, weight):
    frame_total = seq.shape[0]
    out = None
    for p in range(3):
        lag = 2 - p
        if lag >= frame_total:
            continue
        part = conv_rows(seq[: frame_total - lag], weight[p])
        if lag:
            part = jnp.pad(part, ((lag, 0), (0, 0), (0, 0), (0, 0)))
        out = part if out is None else out + part
    return out


def _rms(v, g):
    return v * lax.rsqrt(jnp.mean(v * v, axis=-1, keepdims=True) + epsilon) * g

def _silu(v):
    return v * (1.0 / (1.0 + jnp.exp(-v)))

def block_kernel(cols, frame_count, seq_ref, arrived_ref, swapped_ref, g1_ref, w1_ref, b1_ref, g2_ref,
                 w2_ref, b2_ref, ga_ref, res_ref, normed_ref):
    total = 2 * frame_count
    p_out = seq_ref.shape[1]
    p_mid = p_out + 2 * cols
    first = lax.axis_index("tm") == 0

    def extended(t):
        above = jnp.where(first, arrived_ref[t], swapped_ref[t])
        below = jnp.where(first, swapped_ref[t], arrived_ref[t])
        return jnp.concatenate([above, seq_ref[t], below], axis=0)

    def shifted(a):
        n = a.shape[0]
        col = lax.broadcasted_iota(jnp.int32, (n, 1), 0) % cols
        left = jnp.where(col == 0, 0.0, pltpu.roll(a, 1, 0))
        right = jnp.where(col == cols - 1, 0.0, pltpu.roll(a, n - 1, 0))
        return [left.astype(jnp.bfloat16), a.astype(jnp.bfloat16), right.astype(jnp.bfloat16)]

    def conv_frame(sources, w_ref, out_rows):
        acc = None
        for p, trip in enumerate(sources):
            if trip is None:
                continue
            for q in range(3):
                for s in range(3):
                    window = trip[s][q * cols: q * cols + out_rows]
                    part = jnp.dot(window, w_ref[(p * 3 + q) * 3 + s], preferred_element_type=jnp.float32)
                    acc = part if acc is None else acc + part
        return acc

    g1 = g1_ref[...]
    act1 = [shifted(_silu(_rms(extended(t).astype(jnp.float32), g1)).astype(jnp.bfloat16).astype(jnp.float32)) for t in range(total)]
    inner = lax.axis_size("inner")
    band = lax.axis_index("outer") * inner + lax.axis_index("inner")
    band_rows = p_out // cols
    height = lax.axis_size("outer") * inner * band_rows
    lo = 1 - band * band_rows
    hi = height - band * band_rows + 1
    row = lax.broadcasted_iota(jnp.int32, (p_mid, 1), 0) // cols
    inside = (row >= lo) & (row < hi)
    g2 = g2_ref[...]
    b1 = b1_ref[...]
    act2 = []
    for j in range(total):
        srcs = [act1[j + p - 2] if j + p - 2 >= 0 else None for p in range(3)]
        out1 = conv_frame(srcs, w1_ref, p_mid) + b1
        act2.append(jnp.where(inside, _silu(_rms(out1, g2)), 0.0).astype(jnp.bfloat16).astype(jnp.float32))
    b2 = b2_ref[...]
    ga = ga_ref[...]
    zero = None
    for k in range(frame_count):
        def pick(t_even):
            a = act2[t_even] if 0 <= t_even < total else None
            b = act2[t_even + 1] if 0 <= t_even + 1 < total else None
            if a is None and b is None:
                return None
            a = jnp.zeros_like(act2[0]) if a is None else a
            b = jnp.zeros_like(act2[0]) if b is None else b
            return shifted(jnp.where(first, a, b))
        srcs = [pick(2 * k - 2), pick(2 * k - 1), pick(2 * k)]
        out2 = conv_frame(srcs, w2_ref, p_out) + b2
        own = jnp.where(first, seq_ref[2 * k], seq_ref[2 * k + 1])
        res = own.astype(jnp.float32) + out2
        res_ref[k] = res
        normed_ref[k] = _rms(res, ga).astype(jnp.bfloat16)

def resnet_block(seq, arrived, swapped, g1, w1, b1, g2, w2, b2, ga, cols):
    total, p_out, c = seq.shape
    frame_count = total // 2
    vm = pl.BlockSpec(memory_space=pltpu.VMEM)
    return pl.pallas_call(
        functools.partial(block_kernel, cols, frame_count),
        out_shape=(jax.ShapeDtypeStruct((frame_count, p_out, c), jnp.float32),
                   jax.ShapeDtypeStruct((frame_count, p_out, c), jnp.bfloat16)),
        in_specs=[vm] * 10,
        out_specs=(vm, vm),
    )(seq, arrived, swapped, g1.reshape(1, c), w1.reshape(27, c, c), b1.reshape(1, c), g2.reshape(1, c),
      w2.reshape(27, c, c), b2.reshape(1, c), ga.reshape(1, c))


def local(
    frames,
    norm1_gain,
    conv1_weight,
    conv1_bias,
    norm2_gain,
    conv2_weight,
    conv2_bias,
    attn_gain,
    w_query,
    b_query,
    w_key,
    w_value,
    b_value,
    w_out,
    b_out,
):
    own = frames[:, 0]
    frame_count, row_count, col_count, channels = own.shape
    inner = lax.axis_size("inner")
    bands = lax.axis_size("outer") * inner
    band = lax.axis_index("outer") * inner + lax.axis_index("inner")
    is_first = lax.axis_index("tm") == 0
    height = bands * row_count

    partner = lax.ppermute(own, "tm", [(0, 1), (1, 0)])
    even = jnp.where(is_first, own, partner)
    odd = jnp.where(is_first, partner, own)
    seq = jnp.stack([even, odd], axis=1).reshape(2 * frame_count, row_count, col_count, channels)

    up = [(2 * i, 2 * i + 2) for i in range(bands - 1)]
    down = [(2 * i + 3, 2 * i + 1) for i in range(bands - 1)]
    edge = jnp.where(is_first, seq[:, row_count - HALO :], seq[:, :HALO])
    arrived = lax.ppermute(edge, ("outer", "inner", "tm"), up + down)
    swapped = lax.ppermute(arrived, "tm", [(0, 1), (1, 0)])

    token_count = row_count * col_count
    residual, normed = resnet_block(
        seq.reshape(2 * frame_count, -1, channels),
        arrived.reshape(2 * frame_count, -1, channels),
        swapped.reshape(2 * frame_count, -1, channels),
        norm1_gain,
        conv1_weight,
        conv1_bias,
        norm2_gain,
        conv2_weight,
        conv2_bias,
        attn_gain,
        col_count,
    )
    normed = normed.reshape(frame_count, row_count, col_count, channels)
    flat = normed.reshape(frame_count * token_count, channels)
    query = (jnp.dot(flat, w_query, preferred_element_type=jnp.float32) + b_query).astype(
        jnp.bfloat16
    )
    folded = (
        jnp.dot(query, w_key.T, preferred_element_type=jnp.float32) * (1.0 / math.sqrt(channels))
    ).astype(jnp.bfloat16)
    folded = folded.reshape(frame_count, token_count, channels)

    swap = [(0, 1), (1, 0)]
    partner_queries = lax.ppermute(folded, "inner", swap)
    keys = lax.all_gather(normed, "outer", axis=1, tiled=True)
    keys = keys.reshape(frame_count, -1, channels)
    def partial(queries):
        scores = jnp.einsum("fqc,fkc->fqk", queries, keys, preferred_element_type=jnp.float32)
        top = jnp.max(scores, axis=-1, keepdims=True)
        weights = jnp.exp(scores - top)
        total = jnp.sum(weights, axis=-1, keepdims=True)
        accum = jnp.einsum(
            "fqk,fkc->fqc", weights.astype(jnp.bfloat16), keys, preferred_element_type=jnp.float32
        )
        return jnp.concatenate([accum, top, total], axis=-1)

    returned = lax.ppermute(partial(partner_queries), "inner", swap)
    mine = partial(folded)
    top_mine = mine[..., channels : channels + 1]
    top_back = returned[..., channels : channels + 1]
    highest = jnp.maximum(top_mine, top_back)
    scale_mine = jnp.exp(top_mine - highest)
    scale_back = jnp.exp(top_back - highest)
    total = mine[..., channels + 1 :] * scale_mine + returned[..., channels + 1 :] * scale_back
    accum = mine[..., :channels] * scale_mine + returned[..., :channels] * scale_back
    mixed = (accum / total).astype(jnp.bfloat16).reshape(-1, channels)
    value = (jnp.dot(mixed, w_value, preferred_element_type=jnp.float32) + b_value).astype(
        jnp.bfloat16
    )
    decoded = (
        residual.reshape(-1, channels)
        + jnp.dot(value, w_out, preferred_element_type=jnp.float32)
        + b_out
    )
    return decoded.reshape(frame_count, 1, row_count, col_count, channels)


def solution(mesh):
    clips, bands, cores = mesh.devices.shape
    split = jax.sharding.Mesh(
        mesh.devices.reshape(clips, bands // 2, 2, cores), ("clips", "outer", "inner", "tm")
    )
    banded = P("clips", "tm", ("outer", "inner"), None, None)
    placed = (banded,) + (P(),) * 14
    return jax.shard_map(
        local,
        mesh=split,
        in_specs=placed,
        out_specs=banded,
        check_vma=False,
    )
```

```python
import functools
import math

import jax
import jax.numpy as jnp
from jax import lax
from jax.experimental import pallas as pl
from jax.experimental.layout import Layout, with_layout_constraint
from jax.experimental.pallas import tpu as pltpu
from jax.sharding import PartitionSpec as P

epsilon = 1e-06
HALO = 2


def rms_scale(values, gain):
    return values * lax.rsqrt(jnp.mean(values * values, axis=-1, keepdims=True) + epsilon) * gain


def conv_rows(source, taps):
    return lax.conv_general_dilated(
        source,
        taps,
        window_strides=(1, 1),
        padding=((0, 0), (1, 1)),
        dimension_numbers=("NHWC", "HWIO", "NHWC"),
        preferred_element_type=jnp.float32,
    )


def causal_time_conv(seq, weight):
    frame_total = seq.shape[0]
    out = None
    for p in range(3):
        lag = 2 - p
        if lag >= frame_total:
            continue
        part = conv_rows(seq[: frame_total - lag], weight[p])
        if lag:
            part = jnp.pad(part, ((lag, 0), (0, 0), (0, 0), (0, 0)))
        out = part if out is None else out + part
    return out


def _rms(v, g):
    return v * lax.rsqrt(jnp.mean(v * v, axis=-1, keepdims=True) + epsilon) * g

def _silu(v):
    return v * (1.0 / (1.0 + jnp.exp(-v)))

def block_kernel(cols, frame_count, seq_ref, arrived_ref, swapped_ref, g1_ref, w1_ref, b1_ref, g2_ref,
                 w2_ref, b2_ref, ga_ref, res_ref, normed_ref):
    total = 2 * frame_count
    p_out = seq_ref.shape[1]
    p_mid = p_out + 2 * cols
    first = lax.axis_index("tm") == 0

    def extended(t):
        above = jnp.where(first, arrived_ref[t], swapped_ref[t])
        below = jnp.where(first, swapped_ref[t], arrived_ref[t])
        return jnp.concatenate([above, seq_ref[t], below], axis=0)

    def shifted(a):
        n = a.shape[0]
        col = lax.broadcasted_iota(jnp.int32, (n, 1), 0) % cols
        left = jnp.where(col == 0, 0.0, pltpu.roll(a, 1, 0))
        right = jnp.where(col == cols - 1, 0.0, pltpu.roll(a, n - 1, 0))
        return [left.astype(jnp.bfloat16), a.astype(jnp.bfloat16), right.astype(jnp.bfloat16)]

    def conv_frame(sources, w_ref, out_rows):
        acc = None
        for p, trip in enumerate(sources):
            if trip is None:
                continue
            for q in range(3):
                for s in range(3):
                    window = trip[s][q * cols: q * cols + out_rows]
                    part = jnp.dot(window, w_ref[(p * 3 + q) * 3 + s], preferred_element_type=jnp.float32)
                    acc = part if acc is None else acc + part
        return acc

    g1 = g1_ref[...]
    act1 = [shifted(_silu(_rms(extended(t).astype(jnp.float32), g1)).astype(jnp.bfloat16).astype(jnp.float32)) for t in range(total)]
    inner = lax.axis_size("inner")
    band = lax.axis_index("outer") * inner + lax.axis_index("inner")
    band_rows = p_out // cols
    height = lax.axis_size("outer") * inner * band_rows
    lo = 1 - band * band_rows
    hi = height - band * band_rows + 1
    row = lax.broadcasted_iota(jnp.int32, (p_mid, 1), 0) // cols
    inside = (row >= lo) & (row < hi)
    g2 = g2_ref[...]
    b1 = b1_ref[...]
    act2 = []
    for j in range(total):
        srcs = [act1[j + p - 2] if j + p - 2 >= 0 else None for p in range(3)]
        out1 = conv_frame(srcs, w1_ref, p_mid) + b1
        act2.append(jnp.where(inside, _silu(_rms(out1, g2)), 0.0).astype(jnp.bfloat16).astype(jnp.float32))
    b2 = b2_ref[...]
    ga = ga_ref[...]
    zero = None
    for k in range(frame_count):
        def pick(t_even):
            a = act2[t_even] if 0 <= t_even < total else None
            b = act2[t_even + 1] if 0 <= t_even + 1 < total else None
            if a is None and b is None:
                return None
            a = jnp.zeros_like(act2[0]) if a is None else a
            b = jnp.zeros_like(act2[0]) if b is None else b
            return shifted(jnp.where(first, a, b))
        srcs = [pick(2 * k - 2), pick(2 * k - 1), pick(2 * k)]
        out2 = conv_frame(srcs, w2_ref, p_out) + b2
        own = jnp.where(first, seq_ref[2 * k], seq_ref[2 * k + 1])
        res = own.astype(jnp.float32) + out2
        res_ref[k] = res
        normed_ref[k] = _rms(res, ga).astype(jnp.bfloat16)

def resnet_block(seq, arrived, swapped, g1, w1, b1, g2, w2, b2, ga, cols):
    total, p_out, c = seq.shape
    frame_count = total // 2
    vm = pl.BlockSpec(memory_space=pltpu.VMEM)
    return pl.pallas_call(
        functools.partial(block_kernel, cols, frame_count),
        out_shape=(jax.ShapeDtypeStruct((frame_count, p_out, c), jnp.float32),
                   jax.ShapeDtypeStruct((frame_count, p_out, c), jnp.bfloat16)),
        in_specs=[vm] * 10,
        out_specs=(vm, vm),
    )(seq, arrived, swapped, g1.reshape(1, c), w1.reshape(27, c, c), b1.reshape(1, c), g2.reshape(1, c),
      w2.reshape(27, c, c), b2.reshape(1, c), ga.reshape(1, c))


def local(
    frames,
    norm1_gain,
    conv1_weight,
    conv1_bias,
    norm2_gain,
    conv2_weight,
    conv2_bias,
    attn_gain,
    w_query,
    b_query,
    w_key,
    w_value,
    b_value,
    w_out,
    b_out,
):
    own = with_layout_constraint(frames[:, 0], Layout(major_to_minor=(0, 1, 2, 3)))
    frame_count, row_count, col_count, channels = own.shape
    inner = lax.axis_size("inner")
    bands = lax.axis_size("outer") * inner
    band = lax.axis_index("outer") * inner + lax.axis_index("inner")
    is_first = lax.axis_index("tm") == 0
    height = bands * row_count

    partner = lax.ppermute(own, "tm", [(0, 1), (1, 0)])
    even = jnp.where(is_first, own, partner)
    odd = jnp.where(is_first, partner, own)
    seq = jnp.stack([even, odd], axis=1).reshape(2 * frame_count, row_count, col_count, channels)

    up = [(2 * i, 2 * i + 2) for i in range(bands - 1)]
    down = [(2 * i + 3, 2 * i + 1) for i in range(bands - 1)]
    edge = jnp.where(is_first, seq[:, row_count - HALO :], seq[:, :HALO])
    arrived = lax.ppermute(edge, ("outer", "inner", "tm"), up + down)
    swapped = lax.ppermute(arrived, "tm", [(0, 1), (1, 0)])

    token_count = row_count * col_count
    residual, normed = resnet_block(
        seq.reshape(2 * frame_count, -1, channels),
        arrived.reshape(2 * frame_count, -1, channels),
        swapped.reshape(2 * frame_count, -1, channels),
        norm1_gain,
        conv1_weight,
        conv1_bias,
        norm2_gain,
        conv2_weight,
        conv2_bias,
        attn_gain,
        col_count,
    )
    normed = normed.reshape(frame_count, row_count, col_count, channels)
    flat = normed.reshape(frame_count * token_count, channels)
    query = (jnp.dot(flat, w_query, preferred_element_type=jnp.float32) + b_query).astype(
        jnp.bfloat16
    )
    folded = (
        jnp.dot(query, w_key.T, preferred_element_type=jnp.float32) * (1.0 / math.sqrt(channels))
    ).astype(jnp.bfloat16)
    folded = folded.reshape(frame_count, token_count, channels)

    swap = [(0, 1), (1, 0)]
    partner_queries = lax.ppermute(folded, "inner", swap)
    keys = lax.all_gather(normed, "outer", axis=1, tiled=True)
    keys = keys.reshape(frame_count, -1, channels)
    def partial(queries):
        scores = jnp.einsum("fqc,fkc->fqk", queries, keys, preferred_element_type=jnp.float32)
        top = jnp.max(scores, axis=-1, keepdims=True)
        weights = jnp.exp(scores - top)
        total = jnp.sum(weights, axis=-1, keepdims=True)
        accum = jnp.einsum(
            "fqk,fkc->fqc", weights.astype(jnp.bfloat16), keys, preferred_element_type=jnp.float32
        )
        return jnp.concatenate([accum, top, total], axis=-1)

    returned = lax.ppermute(partial(partner_queries), "inner", swap)
    mine = partial(folded)
    top_mine = mine[..., channels : channels + 1]
    top_back = returned[..., channels : channels + 1]
    highest = jnp.maximum(top_mine, top_back)
    scale_mine = jnp.exp(top_mine - highest)
    scale_back = jnp.exp(top_back - highest)
    total = mine[..., channels + 1 :] * scale_mine + returned[..., channels + 1 :] * scale_back
    accum = mine[..., :channels] * scale_mine + returned[..., :channels] * scale_back
    mixed = (accum / total).astype(jnp.bfloat16).reshape(-1, channels)
    value = (jnp.dot(mixed, w_value, preferred_element_type=jnp.float32) + b_value).astype(
        jnp.bfloat16
    )
    decoded = (
        residual.reshape(-1, channels)
        + jnp.dot(value, w_out, preferred_element_type=jnp.float32)
        + b_out
    )
    return decoded.reshape(frame_count, 1, row_count, col_count, channels)


def solution(mesh):
    clips, bands, cores = mesh.devices.shape
    split = jax.sharding.Mesh(
        mesh.devices.reshape(clips, bands // 2, 2, cores), ("clips", "outer", "inner", "tm")
    )
    banded = P("clips", "tm", ("outer", "inner"), None, None)
    placed = (banded,) + (P(),) * 14
    return jax.shard_map(
        local,
        mesh=split,
        in_specs=placed,
        out_specs=banded,
        check_vma=False,
    )
```

```python
import functools
import math

import jax
import jax.numpy as jnp
from jax import lax
from jax.experimental import pallas as pl
from jax.experimental.layout import Layout, with_layout_constraint
from jax.experimental.pallas import tpu as pltpu
from jax.sharding import PartitionSpec as P

epsilon = 1e-06
HALO = 2


def rms_scale(values, gain):
    return values * lax.rsqrt(jnp.mean(values * values, axis=-1, keepdims=True) + epsilon) * gain


def conv_rows(source, taps):
    return lax.conv_general_dilated(
        source,
        taps,
        window_strides=(1, 1),
        padding=((0, 0), (1, 1)),
        dimension_numbers=("NHWC", "HWIO", "NHWC"),
        preferred_element_type=jnp.float32,
    )


def causal_time_conv(seq, weight):
    frame_total = seq.shape[0]
    out = None
    for p in range(3):
        lag = 2 - p
        if lag >= frame_total:
            continue
        part = conv_rows(seq[: frame_total - lag], weight[p])
        if lag:
            part = jnp.pad(part, ((lag, 0), (0, 0), (0, 0), (0, 0)))
        out = part if out is None else out + part
    return out


def _rms(v, g):
    return v * lax.rsqrt(jnp.mean(v * v, axis=-1, keepdims=True) + epsilon) * g

def _silu(v):
    return v * (1.0 / (1.0 + jnp.exp(-v)))

def block_kernel(cols, frame_count, seq_ref, arrived_ref, swapped_ref, g1_ref, w1_ref, b1_ref, g2_ref,
                 w2_ref, b2_ref, ga_ref, wq_ref, bq_ref, wkt_ref, res_ref, normed_ref, folded_ref):
    total = 2 * frame_count
    p_out = seq_ref.shape[1]
    p_mid = p_out + 2 * cols
    first = lax.axis_index("tm") == 0

    def extended(t):
        above = jnp.where(first, arrived_ref[t], swapped_ref[t])
        below = jnp.where(first, swapped_ref[t], arrived_ref[t])
        return jnp.concatenate([above, seq_ref[t], below], axis=0)

    def shifted(a):
        n = a.shape[0]
        col = lax.broadcasted_iota(jnp.int32, (n, 1), 0) % cols
        left = jnp.where(col == 0, 0.0, pltpu.roll(a, 1, 0))
        right = jnp.where(col == cols - 1, 0.0, pltpu.roll(a, n - 1, 0))
        return [left.astype(jnp.bfloat16), a.astype(jnp.bfloat16), right.astype(jnp.bfloat16)]

    def conv_frame(sources, w_ref, out_rows):
        acc = None
        for p, trip in enumerate(sources):
            if trip is None:
                continue
            for q in range(3):
                for s in range(3):
                    window = trip[s][q * cols: q * cols + out_rows]
                    part = jnp.dot(window, w_ref[(p * 3 + q) * 3 + s], preferred_element_type=jnp.float32)
                    acc = part if acc is None else acc + part
        return acc

    g1 = g1_ref[...]
    act1 = [shifted(_silu(_rms(extended(t).astype(jnp.float32), g1)).astype(jnp.bfloat16).astype(jnp.float32)) for t in range(total)]
    inner = lax.axis_size("inner")
    band = lax.axis_index("outer") * inner + lax.axis_index("inner")
    band_rows = p_out // cols
    height = lax.axis_size("outer") * inner * band_rows
    lo = 1 - band * band_rows
    hi = height - band * band_rows + 1
    row = lax.broadcasted_iota(jnp.int32, (p_mid, 1), 0) // cols
    inside = (row >= lo) & (row < hi)
    g2 = g2_ref[...]
    b1 = b1_ref[...]
    act2 = []
    for j in range(total):
        srcs = [act1[j + p - 2] if j + p - 2 >= 0 else None for p in range(3)]
        out1 = conv_frame(srcs, w1_ref, p_mid) + b1
        act2.append(jnp.where(inside, _silu(_rms(out1, g2)), 0.0).astype(jnp.bfloat16).astype(jnp.float32))
    b2 = b2_ref[...]
    ga = ga_ref[...]
    zero = None
    for k in range(frame_count):
        def pick(t_even):
            a = act2[t_even] if 0 <= t_even < total else None
            b = act2[t_even + 1] if 0 <= t_even + 1 < total else None
            if a is None and b is None:
                return None
            a = jnp.zeros_like(act2[0]) if a is None else a
            b = jnp.zeros_like(act2[0]) if b is None else b
            return shifted(jnp.where(first, a, b))
        srcs = [pick(2 * k - 2), pick(2 * k - 1), pick(2 * k)]
        out2 = conv_frame(srcs, w2_ref, p_out) + b2
        own = jnp.where(first, seq_ref[2 * k], seq_ref[2 * k + 1])
        res = own.astype(jnp.float32) + out2
        res_ref[k] = res
        normed = _rms(res, ga).astype(jnp.bfloat16)
        normed_ref[k] = normed
        query = jnp.dot(normed, wq_ref[...], preferred_element_type=jnp.float32) + bq_ref[...]
        folded = jnp.dot(query.astype(jnp.bfloat16), wkt_ref[...], preferred_element_type=jnp.float32)
        folded_ref[k] = (folded * (1.0 / math.sqrt(res.shape[-1]))).astype(jnp.bfloat16)

def resnet_block(seq, arrived, swapped, g1, w1, b1, g2, w2, b2, ga, wq, bq, wk, cols):
    total, p_out, c = seq.shape
    frame_count = total // 2
    vm = pl.BlockSpec(memory_space=pltpu.VMEM)
    return pl.pallas_call(
        functools.partial(block_kernel, cols, frame_count),
        out_shape=(jax.ShapeDtypeStruct((frame_count, p_out, c), jnp.float32),
                   jax.ShapeDtypeStruct((frame_count, p_out, c), jnp.bfloat16),
                   jax.ShapeDtypeStruct((frame_count, p_out, c), jnp.bfloat16)),
        in_specs=[vm] * 13,
        out_specs=(vm, vm, vm),
    )(seq, arrived, swapped, g1.reshape(1, c), w1.reshape(27, c, c), b1.reshape(1, c), g2.reshape(1, c),
      w2.reshape(27, c, c), b2.reshape(1, c), ga.reshape(1, c), wq, bq.reshape(1, c), wk.T)


def local(
    frames,
    norm1_gain,
    conv1_weight,
    conv1_bias,
    norm2_gain,
    conv2_weight,
    conv2_bias,
    attn_gain,
    w_query,
    b_query,
    w_key,
    w_value,
    b_value,
    w_out,
    b_out,
):
    own = with_layout_constraint(frames[:, 0], Layout(major_to_minor=(0, 1, 2, 3)))
    frame_count, row_count, col_count, channels = own.shape
    inner = lax.axis_size("inner")
    bands = lax.axis_size("outer") * inner
    band = lax.axis_index("outer") * inner + lax.axis_index("inner")
    is_first = lax.axis_index("tm") == 0
    height = bands * row_count

    partner = lax.ppermute(own, "tm", [(0, 1), (1, 0)])
    even = jnp.where(is_first, own, partner)
    odd = jnp.where(is_first, partner, own)
    seq = jnp.stack([even, odd], axis=1).reshape(2 * frame_count, row_count, col_count, channels)

    up = [(2 * i, 2 * i + 2) for i in range(bands - 1)]
    down = [(2 * i + 3, 2 * i + 1) for i in range(bands - 1)]
    edge = jnp.where(is_first, seq[:, row_count - HALO :], seq[:, :HALO])
    arrived = lax.ppermute(edge, ("outer", "inner", "tm"), up + down)
    swapped = lax.ppermute(arrived, "tm", [(0, 1), (1, 0)])

    token_count = row_count * col_count
    residual, normed, folded = resnet_block(
        seq.reshape(2 * frame_count, -1, channels),
        arrived.reshape(2 * frame_count, -1, channels),
        swapped.reshape(2 * frame_count, -1, channels),
        norm1_gain,
        conv1_weight,
        conv1_bias,
        norm2_gain,
        conv2_weight,
        conv2_bias,
        attn_gain,
        w_query,
        b_query,
        w_key,
        col_count,
    )
    normed = normed.reshape(frame_count, row_count, col_count, channels)
    folded = folded.reshape(frame_count, token_count, channels)

    swap = [(0, 1), (1, 0)]
    partner_queries = lax.ppermute(folded, "inner", swap)
    keys = lax.all_gather(normed, "outer", axis=1, tiled=True)
    keys = keys.reshape(frame_count, -1, channels)
    def partial(queries):
        scores = jnp.einsum("fqc,fkc->fqk", queries, keys, preferred_element_type=jnp.float32)
        top = jnp.max(scores, axis=-1, keepdims=True)
        weights = jnp.exp(scores - top)
        total = jnp.sum(weights, axis=-1, keepdims=True)
        accum = jnp.einsum(
            "fqk,fkc->fqc", weights.astype(jnp.bfloat16), keys, preferred_element_type=jnp.float32
        )
        return jnp.concatenate([accum, top, total], axis=-1)

    returned = lax.ppermute(partial(partner_queries), "inner", swap)
    mine = partial(folded)
    top_mine = mine[..., channels : channels + 1]
    top_back = returned[..., channels : channels + 1]
    highest = jnp.maximum(top_mine, top_back)
    scale_mine = jnp.exp(top_mine - highest)
    scale_back = jnp.exp(top_back - highest)
    total = mine[..., channels + 1 :] * scale_mine + returned[..., channels + 1 :] * scale_back
    accum = mine[..., :channels] * scale_mine + returned[..., :channels] * scale_back
    mixed = (accum / total).astype(jnp.bfloat16).reshape(-1, channels)
    value = (jnp.dot(mixed, w_value, preferred_element_type=jnp.float32) + b_value).astype(
        jnp.bfloat16
    )
    decoded = (
        residual.reshape(-1, channels)
        + jnp.dot(value, w_out, preferred_element_type=jnp.float32)
        + b_out
    )
    return decoded.reshape(frame_count, 1, row_count, col_count, channels)


def solution(mesh):
    clips, bands, cores = mesh.devices.shape
    split = jax.sharding.Mesh(
        mesh.devices.reshape(clips, bands // 2, 2, cores), ("clips", "outer", "inner", "tm")
    )
    banded = P("clips", "tm", ("outer", "inner"), None, None)
    placed = (banded,) + (P(),) * 14
    return jax.shard_map(
        local,
        mesh=split,
        in_specs=placed,
        out_specs=banded,
        check_vma=False,
    )
```

```python
import functools
import math

import jax
import jax.numpy as jnp
from jax import lax
from jax.experimental import pallas as pl
from jax.experimental.layout import Layout, with_layout_constraint
from jax.experimental.pallas import tpu as pltpu
from jax.sharding import PartitionSpec as P

epsilon = 1e-06
HALO = 2


def rms_scale(values, gain):
    return values * lax.rsqrt(jnp.mean(values * values, axis=-1, keepdims=True) + epsilon) * gain


def conv_rows(source, taps):
    return lax.conv_general_dilated(
        source,
        taps,
        window_strides=(1, 1),
        padding=((0, 0), (1, 1)),
        dimension_numbers=("NHWC", "HWIO", "NHWC"),
        preferred_element_type=jnp.float32,
    )


def causal_time_conv(seq, weight):
    frame_total = seq.shape[0]
    out = None
    for p in range(3):
        lag = 2 - p
        if lag >= frame_total:
            continue
        part = conv_rows(seq[: frame_total - lag], weight[p])
        if lag:
            part = jnp.pad(part, ((lag, 0), (0, 0), (0, 0), (0, 0)))
        out = part if out is None else out + part
    return out


def _rms(v, g):
    return v * lax.rsqrt(jnp.mean(v * v, axis=-1, keepdims=True) + epsilon) * g

def _silu(v):
    return v * (1.0 / (1.0 + jnp.exp(-v)))

def block_kernel(cols, frame_count, seq_ref, arrived_ref, swapped_ref, g1_ref, w1_ref, b1_ref, g2_ref,
                 w2_ref, b2_ref, ga_ref, wq_ref, bq_ref, wk_ref, res_ref, normed_ref, folded_ref):
    total = 2 * frame_count
    p_out = seq_ref.shape[1]
    p_mid = p_out + 2 * cols
    first = lax.axis_index("tm") == 0

    def extended(t):
        above = jnp.where(first, arrived_ref[t], swapped_ref[t])
        below = jnp.where(first, swapped_ref[t], arrived_ref[t])
        return jnp.concatenate([above, seq_ref[t], below], axis=0)

    def shifted(a):
        n = a.shape[0]
        col = lax.broadcasted_iota(jnp.int32, (n, 1), 0) % cols
        left = jnp.where(col == 0, 0.0, pltpu.roll(a, 1, 0))
        right = jnp.where(col == cols - 1, 0.0, pltpu.roll(a, n - 1, 0))
        return [left.astype(jnp.bfloat16), a.astype(jnp.bfloat16), right.astype(jnp.bfloat16)]

    def conv_frame(sources, w_ref, out_rows):
        acc = None
        for p, trip in enumerate(sources):
            if trip is None:
                continue
            for q in range(3):
                for s in range(3):
                    window = trip[s][q * cols: q * cols + out_rows]
                    part = jnp.dot(window, w_ref[(p * 3 + q) * 3 + s], preferred_element_type=jnp.float32)
                    acc = part if acc is None else acc + part
        return acc

    g1 = g1_ref[...]
    act1 = [shifted(_silu(_rms(extended(t).astype(jnp.float32), g1)).astype(jnp.bfloat16).astype(jnp.float32)) for t in range(total)]
    inner = lax.axis_size("inner")
    band = lax.axis_index("outer") * inner + lax.axis_index("inner")
    band_rows = p_out // cols
    height = lax.axis_size("outer") * inner * band_rows
    lo = 1 - band * band_rows
    hi = height - band * band_rows + 1
    row = lax.broadcasted_iota(jnp.int32, (p_mid, 1), 0) // cols
    inside = (row >= lo) & (row < hi)
    g2 = g2_ref[...]
    b1 = b1_ref[...]
    act2 = []
    for j in range(total):
        srcs = [act1[j + p - 2] if j + p - 2 >= 0 else None for p in range(3)]
        out1 = conv_frame(srcs, w1_ref, p_mid) + b1
        act2.append(jnp.where(inside, _silu(_rms(out1, g2)), 0.0).astype(jnp.bfloat16).astype(jnp.float32))
    b2 = b2_ref[...]
    ga = ga_ref[...]
    zero = None
    for k in range(frame_count):
        def pick(t_even):
            a = act2[t_even] if 0 <= t_even < total else None
            b = act2[t_even + 1] if 0 <= t_even + 1 < total else None
            if a is None and b is None:
                return None
            a = jnp.zeros_like(act2[0]) if a is None else a
            b = jnp.zeros_like(act2[0]) if b is None else b
            return shifted(jnp.where(first, a, b))
        srcs = [pick(2 * k - 2), pick(2 * k - 1), pick(2 * k)]
        out2 = conv_frame(srcs, w2_ref, p_out) + b2
        own = jnp.where(first, seq_ref[2 * k], seq_ref[2 * k + 1])
        res = own.astype(jnp.float32) + out2
        res_ref[k] = res
        normed = _rms(res, ga).astype(jnp.bfloat16)
        normed_ref[k] = normed
        query = jnp.dot(normed, wq_ref[...], preferred_element_type=jnp.float32) + bq_ref[...]
        folded = lax.dot_general(
            query.astype(jnp.bfloat16), wk_ref[...], (((1,), (1,)), ((), ())),
            preferred_element_type=jnp.float32,
        )
        folded_ref[k] = (folded * (1.0 / math.sqrt(res.shape[-1]))).astype(jnp.bfloat16)

def resnet_block(seq, arrived, swapped, g1, w1, b1, g2, w2, b2, ga, wq, bq, wk, cols):
    total, p_out, c = seq.shape
    frame_count = total // 2
    vm = pl.BlockSpec(memory_space=pltpu.VMEM)
    return pl.pallas_call(
        functools.partial(block_kernel, cols, frame_count),
        out_shape=(jax.ShapeDtypeStruct((frame_count, p_out, c), jnp.float32),
                   jax.ShapeDtypeStruct((frame_count, p_out, c), jnp.bfloat16),
                   jax.ShapeDtypeStruct((frame_count, p_out, c), jnp.bfloat16)),
        in_specs=[vm] * 13,
        out_specs=(vm, vm, vm),
    )(seq, arrived, swapped, g1.reshape(1, c), w1.reshape(27, c, c), b1.reshape(1, c), g2.reshape(1, c),
      w2.reshape(27, c, c), b2.reshape(1, c), ga.reshape(1, c), wq, bq.reshape(1, c), wk)


def local(
    frames,
    norm1_gain,
    conv1_weight,
    conv1_bias,
    norm2_gain,
    conv2_weight,
    conv2_bias,
    attn_gain,
    w_query,
    b_query,
    w_key,
    w_value,
    b_value,
    w_out,
    b_out,
):
    own = with_layout_constraint(frames[:, 0], Layout(major_to_minor=(0, 1, 2, 3)))
    frame_count, row_count, col_count, channels = own.shape
    inner = lax.axis_size("inner")
    bands = lax.axis_size("outer") * inner
    band = lax.axis_index("outer") * inner + lax.axis_index("inner")
    is_first = lax.axis_index("tm") == 0
    height = bands * row_count

    partner = lax.ppermute(own, "tm", [(0, 1), (1, 0)])
    even = jnp.where(is_first, own, partner)
    odd = jnp.where(is_first, partner, own)
    seq = jnp.stack([even, odd], axis=1).reshape(2 * frame_count, row_count, col_count, channels)

    up = [(2 * i, 2 * i + 2) for i in range(bands - 1)]
    down = [(2 * i + 3, 2 * i + 1) for i in range(bands - 1)]
    edge = jnp.where(is_first, seq[:, row_count - HALO :], seq[:, :HALO])
    arrived = lax.ppermute(edge, ("outer", "inner", "tm"), up + down)
    swapped = lax.ppermute(arrived, "tm", [(0, 1), (1, 0)])

    token_count = row_count * col_count
    residual, normed, folded = resnet_block(
        seq.reshape(2 * frame_count, -1, channels),
        arrived.reshape(2 * frame_count, -1, channels),
        swapped.reshape(2 * frame_count, -1, channels),
        norm1_gain,
        conv1_weight,
        conv1_bias,
        norm2_gain,
        conv2_weight,
        conv2_bias,
        attn_gain,
        w_query,
        b_query,
        w_key,
        col_count,
    )
    normed = normed.reshape(frame_count, row_count, col_count, channels)
    folded = folded.reshape(frame_count, token_count, channels)

    swap = [(0, 1), (1, 0)]
    partner_queries = lax.ppermute(folded, "inner", swap)
    keys = lax.all_gather(normed, "outer", axis=1, tiled=True)
    keys = keys.reshape(frame_count, -1, channels)
    def partial(queries):
        scores = jnp.einsum("fqc,fkc->fqk", queries, keys, preferred_element_type=jnp.float32)
        top = jnp.max(scores, axis=-1, keepdims=True)
        weights = jnp.exp(scores - top)
        total = jnp.sum(weights, axis=-1, keepdims=True)
        accum = jnp.einsum(
            "fqk,fkc->fqc", weights.astype(jnp.bfloat16), keys, preferred_element_type=jnp.float32
        )
        return jnp.concatenate([accum, top, total], axis=-1)

    returned = lax.ppermute(partial(partner_queries), "inner", swap)
    mine = partial(folded)
    top_mine = mine[..., channels : channels + 1]
    top_back = returned[..., channels : channels + 1]
    highest = jnp.maximum(top_mine, top_back)
    scale_mine = jnp.exp(top_mine - highest)
    scale_back = jnp.exp(top_back - highest)
    total = mine[..., channels + 1 :] * scale_mine + returned[..., channels + 1 :] * scale_back
    accum = mine[..., :channels] * scale_mine + returned[..., :channels] * scale_back
    mixed = (accum / total).astype(jnp.bfloat16).reshape(-1, channels)
    value = (jnp.dot(mixed, w_value, preferred_element_type=jnp.float32) + b_value).astype(
        jnp.bfloat16
    )
    decoded = (
        residual.reshape(-1, channels)
        + jnp.dot(value, w_out, preferred_element_type=jnp.float32)
        + b_out
    )
    return decoded.reshape(frame_count, 1, row_count, col_count, channels)


def solution(mesh):
    clips, bands, cores = mesh.devices.shape
    split = jax.sharding.Mesh(
        mesh.devices.reshape(clips, bands // 2, 2, cores), ("clips", "outer", "inner", "tm")
    )
    banded = P("clips", "tm", ("outer", "inner"), None, None)
    placed = (banded,) + (P(),) * 14
    return jax.shard_map(
        local,
        mesh=split,
        in_specs=placed,
        out_specs=banded,
        check_vma=False,
    )
```

```python
import functools
import math

import jax
import jax.numpy as jnp
from jax import lax
from jax.experimental import pallas as pl
from jax.experimental.layout import Layout, with_layout_constraint
from jax.experimental.pallas import tpu as pltpu
from jax.sharding import PartitionSpec as P

epsilon = 1e-06
HALO = 2


def rms_scale(values, gain):
    return values * lax.rsqrt(jnp.mean(values * values, axis=-1, keepdims=True) + epsilon) * gain


def conv_rows(source, taps):
    return lax.conv_general_dilated(
        source,
        taps,
        window_strides=(1, 1),
        padding=((0, 0), (1, 1)),
        dimension_numbers=("NHWC", "HWIO", "NHWC"),
        preferred_element_type=jnp.float32,
    )


def causal_time_conv(seq, weight):
    frame_total = seq.shape[0]
    out = None
    for p in range(3):
        lag = 2 - p
        if lag >= frame_total:
            continue
        part = conv_rows(seq[: frame_total - lag], weight[p])
        if lag:
            part = jnp.pad(part, ((lag, 0), (0, 0), (0, 0), (0, 0)))
        out = part if out is None else out + part
    return out


def _rms(v, g):
    return v * lax.rsqrt(jnp.mean(v * v, axis=-1, keepdims=True) + epsilon) * g

def _silu(v):
    return v * (1.0 / (1.0 + jnp.exp(-v)))

def block_kernel(cols, frame_count, seq_ref, arrived_ref, swapped_ref, g1_ref, w1_ref, b1_ref, g2_ref,
                 w2_ref, b2_ref, ga_ref, wq_ref, bq_ref, wk_ref, res_ref, normed_ref, folded_ref):
    total = 2 * frame_count
    p_out = seq_ref.shape[1]
    p_mid = p_out + 2 * cols
    first = lax.axis_index("tm") == 0

    def extended(t):
        above = jnp.where(first, arrived_ref[t], swapped_ref[t])
        below = jnp.where(first, swapped_ref[t], arrived_ref[t])
        return jnp.concatenate([above, seq_ref[t], below], axis=0)

    def shifted(a):
        n = a.shape[0]
        col = lax.broadcasted_iota(jnp.int32, (n, 1), 0) % cols
        left = jnp.where(col == 0, 0.0, pltpu.roll(a, 1, 0))
        right = jnp.where(col == cols - 1, 0.0, pltpu.roll(a, n - 1, 0))
        return [left.astype(jnp.bfloat16), a.astype(jnp.bfloat16), right.astype(jnp.bfloat16)]

    def conv_frame(sources, w_ref, out_rows):
        acc = None
        for p, trip in enumerate(sources):
            if trip is None:
                continue
            for q in range(3):
                for s in range(3):
                    window = trip[s][q * cols: q * cols + out_rows]
                    part = jnp.dot(window, w_ref[(p * 3 + q) * 3 + s], preferred_element_type=jnp.float32)
                    acc = part if acc is None else acc + part
        return acc

    g1 = g1_ref[...]
    act1 = [shifted(_silu(_rms(extended(t).astype(jnp.float32), g1)).astype(jnp.bfloat16).astype(jnp.float32)) for t in range(total)]
    inner = lax.axis_size("inner")
    band = lax.axis_index("outer") * inner + lax.axis_index("inner")
    band_rows = p_out // cols
    height = lax.axis_size("outer") * inner * band_rows
    lo = 1 - band * band_rows
    hi = height - band * band_rows + 1
    row = lax.broadcasted_iota(jnp.int32, (p_mid, 1), 0) // cols
    inside = (row >= lo) & (row < hi)
    g2 = g2_ref[...]
    b1 = b1_ref[...]
    acc = [None] * total
    for p in range(3):
        outs = [j for j in range(total) if j + p - 2 >= 0]
        if not outs:
            continue
        for q in range(3):
            for s in range(3):
                pieces = [act1[j + p - 2][s][q * cols: q * cols + p_mid] for j in outs]
                window = pieces[0] if len(pieces) == 1 else jnp.concatenate(pieces, axis=0)
                part = jnp.dot(window, w1_ref[(p * 3 + q) * 3 + s], preferred_element_type=jnp.float32)
                for i, j in enumerate(outs):
                    piece = part[i * p_mid: (i + 1) * p_mid]
                    acc[j] = piece if acc[j] is None else acc[j] + piece
    act2 = []
    for j in range(total):
        out1 = acc[j] + b1
        act2.append(jnp.where(inside, _silu(_rms(out1, g2)), 0.0).astype(jnp.bfloat16).astype(jnp.float32))
    b2 = b2_ref[...]
    ga = ga_ref[...]
    zero = None
    for k in range(frame_count):
        def pick(t_even):
            a = act2[t_even] if 0 <= t_even < total else None
            b = act2[t_even + 1] if 0 <= t_even + 1 < total else None
            if a is None and b is None:
                return None
            a = jnp.zeros_like(act2[0]) if a is None else a
            b = jnp.zeros_like(act2[0]) if b is None else b
            return shifted(jnp.where(first, a, b))
        srcs = [pick(2 * k - 2), pick(2 * k - 1), pick(2 * k)]
        out2 = conv_frame(srcs, w2_ref, p_out) + b2
        own = jnp.where(first, seq_ref[2 * k], seq_ref[2 * k + 1])
        res = own.astype(jnp.float32) + out2
        res_ref[k] = res
        normed = _rms(res, ga).astype(jnp.bfloat16)
        normed_ref[k] = normed
        query = jnp.dot(normed, wq_ref[...], preferred_element_type=jnp.float32) + bq_ref[...]
        folded = lax.dot_general(
            query.astype(jnp.bfloat16), wk_ref[...], (((1,), (1,)), ((), ())),
            preferred_element_type=jnp.float32,
        )
        folded_ref[k] = (folded * (1.0 / math.sqrt(res.shape[-1]))).astype(jnp.bfloat16)

def resnet_block(seq, arrived, swapped, g1, w1, b1, g2, w2, b2, ga, wq, bq, wk, cols):
    total, p_out, c = seq.shape
    frame_count = total // 2
    vm = pl.BlockSpec(memory_space=pltpu.VMEM)
    return pl.pallas_call(
        functools.partial(block_kernel, cols, frame_count),
        out_shape=(jax.ShapeDtypeStruct((frame_count, p_out, c), jnp.float32),
                   jax.ShapeDtypeStruct((frame_count, p_out, c), jnp.bfloat16),
                   jax.ShapeDtypeStruct((frame_count, p_out, c), jnp.bfloat16)),
        in_specs=[vm] * 13,
        out_specs=(vm, vm, vm),
    )(seq, arrived, swapped, g1.reshape(1, c), w1.reshape(27, c, c), b1.reshape(1, c), g2.reshape(1, c),
      w2.reshape(27, c, c), b2.reshape(1, c), ga.reshape(1, c), wq, bq.reshape(1, c), wk)


def local(
    frames,
    norm1_gain,
    conv1_weight,
    conv1_bias,
    norm2_gain,
    conv2_weight,
    conv2_bias,
    attn_gain,
    w_query,
    b_query,
    w_key,
    w_value,
    b_value,
    w_out,
    b_out,
):
    own = with_layout_constraint(frames[:, 0], Layout(major_to_minor=(0, 1, 2, 3)))
    frame_count, row_count, col_count, channels = own.shape
    inner = lax.axis_size("inner")
    bands = lax.axis_size("outer") * inner
    band = lax.axis_index("outer") * inner + lax.axis_index("inner")
    is_first = lax.axis_index("tm") == 0
    height = bands * row_count

    partner = lax.ppermute(own, "tm", [(0, 1), (1, 0)])
    even = jnp.where(is_first, own, partner)
    odd = jnp.where(is_first, partner, own)
    seq = jnp.stack([even, odd], axis=1).reshape(2 * frame_count, row_count, col_count, channels)

    up = [(2 * i, 2 * i + 2) for i in range(bands - 1)]
    down = [(2 * i + 3, 2 * i + 1) for i in range(bands - 1)]
    edge = jnp.where(is_first, seq[:, row_count - HALO :], seq[:, :HALO])
    arrived = lax.ppermute(edge, ("outer", "inner", "tm"), up + down)
    swapped = lax.ppermute(arrived, "tm", [(0, 1), (1, 0)])

    token_count = row_count * col_count
    residual, normed, folded = resnet_block(
        seq.reshape(2 * frame_count, -1, channels),
        arrived.reshape(2 * frame_count, -1, channels),
        swapped.reshape(2 * frame_count, -1, channels),
        norm1_gain,
        conv1_weight,
        conv1_bias,
        norm2_gain,
        conv2_weight,
        conv2_bias,
        attn_gain,
        w_query,
        b_query,
        w_key,
        col_count,
    )
    normed = normed.reshape(frame_count, row_count, col_count, channels)
    folded = folded.reshape(frame_count, token_count, channels)

    swap = [(0, 1), (1, 0)]
    partner_queries = lax.ppermute(folded, "inner", swap)
    keys = lax.all_gather(normed, "outer", axis=1, tiled=True)
    keys = keys.reshape(frame_count, -1, channels)
    def partial(queries):
        scores = jnp.einsum("fqc,fkc->fqk", queries, keys, preferred_element_type=jnp.float32)
        top = jnp.max(scores, axis=-1, keepdims=True)
        weights = jnp.exp(scores - top)
        total = jnp.sum(weights, axis=-1, keepdims=True)
        accum = jnp.einsum(
            "fqk,fkc->fqc", weights.astype(jnp.bfloat16), keys, preferred_element_type=jnp.float32
        )
        return jnp.concatenate([accum, top, total], axis=-1)

    returned = lax.ppermute(partial(partner_queries), "inner", swap)
    mine = partial(folded)
    top_mine = mine[..., channels : channels + 1]
    top_back = returned[..., channels : channels + 1]
    highest = jnp.maximum(top_mine, top_back)
    scale_mine = jnp.exp(top_mine - highest)
    scale_back = jnp.exp(top_back - highest)
    total = mine[..., channels + 1 :] * scale_mine + returned[..., channels + 1 :] * scale_back
    accum = mine[..., :channels] * scale_mine + returned[..., :channels] * scale_back
    mixed = (accum / total).astype(jnp.bfloat16).reshape(-1, channels)
    value = (jnp.dot(mixed, w_value, preferred_element_type=jnp.float32) + b_value).astype(
        jnp.bfloat16
    )
    decoded = (
        residual.reshape(-1, channels)
        + jnp.dot(value, w_out, preferred_element_type=jnp.float32)
        + b_out
    )
    return decoded.reshape(frame_count, 1, row_count, col_count, channels)


def solution(mesh):
    clips, bands, cores = mesh.devices.shape
    split = jax.sharding.Mesh(
        mesh.devices.reshape(clips, bands // 2, 2, cores), ("clips", "outer", "inner", "tm")
    )
    banded = P("clips", "tm", ("outer", "inner"), None, None)
    placed = (banded,) + (P(),) * 14
    return jax.shard_map(
        local,
        mesh=split,
        in_specs=placed,
        out_specs=banded,
        check_vma=False,
    )
```

```python
import functools
import math

import jax
import jax.numpy as jnp
from jax import lax
from jax.experimental import pallas as pl
from jax.experimental.layout import Layout, with_layout_constraint
from jax.experimental.pallas import tpu as pltpu
from jax.sharding import PartitionSpec as P

epsilon = 1e-06
HALO = 2


def rms_scale(values, gain):
    return values * lax.rsqrt(jnp.mean(values * values, axis=-1, keepdims=True) + epsilon) * gain


def conv_rows(source, taps):
    return lax.conv_general_dilated(
        source,
        taps,
        window_strides=(1, 1),
        padding=((0, 0), (1, 1)),
        dimension_numbers=("NHWC", "HWIO", "NHWC"),
        preferred_element_type=jnp.float32,
    )


def causal_time_conv(seq, weight):
    frame_total = seq.shape[0]
    out = None
    for p in range(3):
        lag = 2 - p
        if lag >= frame_total:
            continue
        part = conv_rows(seq[: frame_total - lag], weight[p])
        if lag:
            part = jnp.pad(part, ((lag, 0), (0, 0), (0, 0), (0, 0)))
        out = part if out is None else out + part
    return out


def _rms(v, g):
    return v * lax.rsqrt(jnp.mean(v * v, axis=-1, keepdims=True) + epsilon) * g

def _silu(v):
    return v * (1.0 / (1.0 + jnp.exp(-v)))

def block_kernel(cols, frame_count, seq_ref, arrived_ref, swapped_ref, g1_ref, w1_ref, b1_ref, g2_ref,
                 w2_ref, b2_ref, ga_ref, wq_ref, bq_ref, wk_ref, res_ref, normed_ref, folded_ref):
    total = 2 * frame_count
    p_out = seq_ref.shape[1]
    p_mid = p_out + 2 * cols
    first = lax.axis_index("tm") == 0

    def extended(t):
        above = jnp.where(first, arrived_ref[t], swapped_ref[t])
        below = jnp.where(first, swapped_ref[t], arrived_ref[t])
        return jnp.concatenate([above, seq_ref[t], below], axis=0)

    def shifted(a):
        n = a.shape[0]
        col = lax.broadcasted_iota(jnp.int32, (n, 1), 0) % cols
        left = jnp.where(col == 0, 0.0, pltpu.roll(a, 1, 0))
        right = jnp.where(col == cols - 1, 0.0, pltpu.roll(a, n - 1, 0))
        return [left.astype(jnp.bfloat16), a.astype(jnp.bfloat16), right.astype(jnp.bfloat16)]

    def conv_frame(sources, w_ref, out_rows):
        acc = None
        for p, trip in enumerate(sources):
            if trip is None:
                continue
            for q in range(3):
                for s in range(3):
                    window = trip[s][q * cols: q * cols + out_rows]
                    part = jnp.dot(window, w_ref[(p * 3 + q) * 3 + s], preferred_element_type=jnp.float32)
                    acc = part if acc is None else acc + part
        return acc

    g1 = g1_ref[...]
    act1 = [shifted(_silu(_rms(extended(t).astype(jnp.float32), g1)).astype(jnp.bfloat16).astype(jnp.float32)) for t in range(total)]
    inner = lax.axis_size("inner")
    band = lax.axis_index("outer") * inner + lax.axis_index("inner")
    band_rows = p_out // cols
    height = lax.axis_size("outer") * inner * band_rows
    lo = 1 - band * band_rows
    hi = height - band * band_rows + 1
    row = lax.broadcasted_iota(jnp.int32, (p_mid, 1), 0) // cols
    inside = (row >= lo) & (row < hi)
    g2 = g2_ref[...]
    b1 = b1_ref[...]
    act2 = []
    for j in range(total):
        srcs = [act1[j + p - 2] if j + p - 2 >= 0 else None for p in range(3)]
        out1 = conv_frame(srcs, w1_ref, p_mid) + b1
        act2.append(jnp.where(inside, _silu(_rms(out1, g2)), 0.0).astype(jnp.bfloat16).astype(jnp.float32))
    b2 = b2_ref[...]
    ga = ga_ref[...]
    zero = None
    for k in range(frame_count):
        def pick(t_even):
            a = act2[t_even] if 0 <= t_even < total else None
            b = act2[t_even + 1] if 0 <= t_even + 1 < total else None
            if a is None and b is None:
                return None
            a = jnp.zeros_like(act2[0]) if a is None else a
            b = jnp.zeros_like(act2[0]) if b is None else b
            return shifted(jnp.where(first, a, b))
        srcs = [pick(2 * k - 2), pick(2 * k - 1), pick(2 * k)]
        out2 = conv_frame(srcs, w2_ref, p_out) + b2
        own = jnp.where(first, seq_ref[2 * k], seq_ref[2 * k + 1])
        res = own.astype(jnp.float32) + out2
        res_ref[k] = res
        normed = _rms(res, ga).astype(jnp.bfloat16)
        normed_ref[k] = normed
        query = jnp.dot(normed, wq_ref[...], preferred_element_type=jnp.float32) + bq_ref[...]
        folded = lax.dot_general(
            query.astype(jnp.bfloat16), wk_ref[...], (((1,), (1,)), ((), ())),
            preferred_element_type=jnp.float32,
        )
        folded_ref[k] = (folded * (1.0 / math.sqrt(res.shape[-1]))).astype(jnp.bfloat16)

def resnet_block(seq, arrived, swapped, g1, w1, b1, g2, w2, b2, ga, wq, bq, wk, cols):
    total, p_out, c = seq.shape
    frame_count = total // 2
    vm = pl.BlockSpec(memory_space=pltpu.VMEM)
    return pl.pallas_call(
        functools.partial(block_kernel, cols, frame_count),
        out_shape=(jax.ShapeDtypeStruct((frame_count, p_out, c), jnp.float32),
                   jax.ShapeDtypeStruct((frame_count, p_out, c), jnp.bfloat16),
                   jax.ShapeDtypeStruct((frame_count, p_out, c), jnp.bfloat16)),
        in_specs=[vm] * 13,
        out_specs=(vm, vm, vm),
    )(seq, arrived, swapped, g1.reshape(1, c), w1.reshape(27, c, c), b1.reshape(1, c), g2.reshape(1, c),
      w2.reshape(27, c, c), b2.reshape(1, c), ga.reshape(1, c), wq, bq.reshape(1, c), wk)


def local(
    frames,
    norm1_gain,
    conv1_weight,
    conv1_bias,
    norm2_gain,
    conv2_weight,
    conv2_bias,
    attn_gain,
    w_query,
    b_query,
    w_key,
    w_value,
    b_value,
    w_out,
    b_out,
):
    own = with_layout_constraint(frames[:, 0], Layout(major_to_minor=(0, 1, 2, 3)))
    frame_count, row_count, col_count, channels = own.shape
    inner = lax.axis_size("inner")
    bands = lax.axis_size("outer") * inner
    band = lax.axis_index("outer") * inner + lax.axis_index("inner")
    is_first = lax.axis_index("tm") == 0
    height = bands * row_count

    partner = lax.ppermute(own, "tm", [(0, 1), (1, 0)])
    even = jnp.where(is_first, own, partner)
    odd = jnp.where(is_first, partner, own)
    seq = jnp.stack([even, odd], axis=1).reshape(2 * frame_count, row_count, col_count, channels)

    up = [(2 * i, 2 * i + 2) for i in range(bands - 1)]
    down = [(2 * i + 3, 2 * i + 1) for i in range(bands - 1)]
    edge = jnp.where(is_first, seq[:, row_count - HALO :], seq[:, :HALO])
    arrived = lax.ppermute(edge, ("outer", "inner", "tm"), up + down)
    swapped = lax.ppermute(arrived, "tm", [(0, 1), (1, 0)])

    token_count = row_count * col_count
    residual, normed, folded = resnet_block(
        seq.reshape(2 * frame_count, -1, channels),
        arrived.reshape(2 * frame_count, -1, channels),
        swapped.reshape(2 * frame_count, -1, channels),
        norm1_gain,
        conv1_weight,
        conv1_bias,
        norm2_gain,
        conv2_weight,
        conv2_bias,
        attn_gain,
        w_query,
        b_query,
        w_key,
        col_count,
    )
    normed = normed.reshape(frame_count, row_count, col_count, channels)
    folded = folded.reshape(frame_count, token_count, channels)

    swap = [(0, 1), (1, 0)]
    partner_queries = lax.ppermute(folded, "inner", swap)
    keys = lax.all_gather(normed, "outer", axis=1, tiled=True)
    keys = keys.reshape(frame_count, -1, channels)
    def partial(queries):
        scores = jnp.einsum("fqc,fkc->fqk", queries, keys, preferred_element_type=jnp.float32)
        top = jnp.max(scores, axis=-1, keepdims=True)
        weights = jnp.exp(scores - top)
        total = jnp.sum(weights, axis=-1, keepdims=True)
        accum = jnp.einsum(
            "fqk,fkc->fqc", weights.astype(jnp.bfloat16), keys, preferred_element_type=jnp.float32
        )
        return accum, jnp.concatenate([top, total], axis=-1)

    back_accum, back_stats = partial(partner_queries)
    returned_accum, returned_stats = lax.ppermute(
        (back_accum.astype(jnp.bfloat16), back_stats), "inner", swap
    )
    mine_accum, mine_stats = partial(folded)
    top_mine = mine_stats[..., :1]
    top_back = returned_stats[..., :1]
    highest = jnp.maximum(top_mine, top_back)
    scale_mine = jnp.exp(top_mine - highest)
    scale_back = jnp.exp(top_back - highest)
    total = mine_stats[..., 1:] * scale_mine + returned_stats[..., 1:] * scale_back
    accum = mine_accum * scale_mine + returned_accum.astype(jnp.float32) * scale_back
    mixed = (accum / total).astype(jnp.bfloat16).reshape(-1, channels)
    value = (jnp.dot(mixed, w_value, preferred_element_type=jnp.float32) + b_value).astype(
        jnp.bfloat16
    )
    decoded = (
        residual.reshape(-1, channels)
        + jnp.dot(value, w_out, preferred_element_type=jnp.float32)
        + b_out
    )
    return decoded.reshape(frame_count, 1, row_count, col_count, channels)


def solution(mesh):
    clips, bands, cores = mesh.devices.shape
    split = jax.sharding.Mesh(
        mesh.devices.reshape(clips, bands // 2, 2, cores), ("clips", "outer", "inner", "tm")
    )
    banded = P("clips", "tm", ("outer", "inner"), None, None)
    placed = (banded,) + (P(),) * 14
    return jax.shard_map(
        local,
        mesh=split,
        in_specs=placed,
        out_specs=banded,
        check_vma=False,
    )
```

```python
import functools
import math

import jax
import jax.numpy as jnp
from jax import lax
from jax.experimental import pallas as pl
from jax.experimental.layout import Layout, with_layout_constraint
from jax.experimental.pallas import tpu as pltpu
from jax.sharding import PartitionSpec as P

epsilon = 1e-06
HALO = 2


def rms_scale(values, gain):
    return values * lax.rsqrt(jnp.mean(values * values, axis=-1, keepdims=True) + epsilon) * gain


def conv_rows(source, taps):
    return lax.conv_general_dilated(
        source,
        taps,
        window_strides=(1, 1),
        padding=((0, 0), (1, 1)),
        dimension_numbers=("NHWC", "HWIO", "NHWC"),
        preferred_element_type=jnp.float32,
    )


def causal_time_conv(seq, weight):
    frame_total = seq.shape[0]
    out = None
    for p in range(3):
        lag = 2 - p
        if lag >= frame_total:
            continue
        part = conv_rows(seq[: frame_total - lag], weight[p])
        if lag:
            part = jnp.pad(part, ((lag, 0), (0, 0), (0, 0), (0, 0)))
        out = part if out is None else out + part
    return out


def _rms(v, g):
    return v * lax.rsqrt(jnp.mean(v * v, axis=-1, keepdims=True) + epsilon) * g

def _silu(v):
    return v * (1.0 / (1.0 + jnp.exp(-v)))

def block_kernel(cols, frame_count, seq_ref, arrived_ref, swapped_ref, g1_ref, w1_ref, b1_ref, g2_ref,
                 w2_ref, b2_ref, ga_ref, wq_ref, bq_ref, wk_ref, res_ref, normed_ref, folded_ref):
    total = 2 * frame_count
    p_out = seq_ref.shape[1]
    p_mid = p_out + 2 * cols
    first = lax.axis_index("tm") == 0

    def extended(t):
        above = jnp.where(first, arrived_ref[t], swapped_ref[t])
        below = jnp.where(first, swapped_ref[t], arrived_ref[t])
        return jnp.concatenate([above, seq_ref[t], below], axis=0)

    def shifted(a):
        n = a.shape[0]
        col = lax.broadcasted_iota(jnp.int32, (n, 1), 0) % cols
        left = jnp.where(col == 0, 0.0, pltpu.roll(a, 1, 0))
        right = jnp.where(col == cols - 1, 0.0, pltpu.roll(a, n - 1, 0))
        return [left.astype(jnp.bfloat16), a.astype(jnp.bfloat16), right.astype(jnp.bfloat16)]

    def conv_frame(sources, w_ref, out_rows):
        acc = None
        for p, trip in enumerate(sources):
            if trip is None:
                continue
            for q in range(3):
                for s in range(3):
                    window = trip[s][q * cols: q * cols + out_rows]
                    part = jnp.dot(window, w_ref[(p * 3 + q) * 3 + s], preferred_element_type=jnp.float32)
                    acc = part if acc is None else acc + part
        return acc

    g1 = g1_ref[...]
    act1 = [shifted(_silu(_rms(extended(t).astype(jnp.float32), g1)).astype(jnp.bfloat16).astype(jnp.float32)) for t in range(total)]
    inner = lax.axis_size("inner")
    band = lax.axis_index("outer") * inner + lax.axis_index("inner")
    band_rows = p_out // cols
    height = lax.axis_size("outer") * inner * band_rows
    lo = 1 - band * band_rows
    hi = height - band * band_rows + 1
    row = lax.broadcasted_iota(jnp.int32, (p_mid, 1), 0) // cols
    inside = (row >= lo) & (row < hi)
    g2 = g2_ref[...]
    b1 = b1_ref[...]
    act2 = []
    for j in range(total):
        srcs = [act1[j + p - 2] if j + p - 2 >= 0 else None for p in range(3)]
        out1 = conv_frame(srcs, w1_ref, p_mid) + b1
        act2.append(jnp.where(inside, _silu(_rms(out1, g2)), 0.0).astype(jnp.bfloat16).astype(jnp.float32))
    b2 = b2_ref[...]
    ga = ga_ref[...]
    zero = None
    for k in range(frame_count):
        def pick(t_even):
            a = act2[t_even] if 0 <= t_even < total else None
            b = act2[t_even + 1] if 0 <= t_even + 1 < total else None
            if a is None and b is None:
                return None
            a = jnp.zeros_like(act2[0]) if a is None else a
            b = jnp.zeros_like(act2[0]) if b is None else b
            return shifted(jnp.where(first, a, b))
        srcs = [pick(2 * k - 2), pick(2 * k - 1), pick(2 * k)]
        out2 = conv_frame(srcs, w2_ref, p_out) + b2
        own = jnp.where(first, seq_ref[2 * k], seq_ref[2 * k + 1])
        res = own.astype(jnp.float32) + out2
        res_ref[k] = res
        normed = _rms(res, ga).astype(jnp.bfloat16)
        normed_ref[k] = normed
        query = jnp.dot(normed, wq_ref[...], preferred_element_type=jnp.float32) + bq_ref[...]
        folded = lax.dot_general(
            query.astype(jnp.bfloat16), wk_ref[...], (((1,), (1,)), ((), ())),
            preferred_element_type=jnp.float32,
        )
        folded_ref[k] = (folded * (1.0 / math.sqrt(res.shape[-1]))).astype(jnp.bfloat16)

def resnet_block(seq, arrived, swapped, g1, w1, b1, g2, w2, b2, ga, wq, bq, wk, cols):
    total, p_out, c = seq.shape
    frame_count = total // 2
    vm = pl.BlockSpec(memory_space=pltpu.VMEM)
    return pl.pallas_call(
        functools.partial(block_kernel, cols, frame_count),
        out_shape=(jax.ShapeDtypeStruct((frame_count, p_out, c), jnp.float32),
                   jax.ShapeDtypeStruct((frame_count, p_out, c), jnp.bfloat16),
                   jax.ShapeDtypeStruct((frame_count, p_out, c), jnp.bfloat16)),
        in_specs=[vm] * 13,
        out_specs=(vm, vm, vm),
    )(seq, arrived, swapped, g1.reshape(1, c), w1.reshape(27, c, c), b1.reshape(1, c), g2.reshape(1, c),
      w2.reshape(27, c, c), b2.reshape(1, c), ga.reshape(1, c), wq, bq.reshape(1, c), wk)


def local(
    frames,
    norm1_gain,
    conv1_weight,
    conv1_bias,
    norm2_gain,
    conv2_weight,
    conv2_bias,
    attn_gain,
    w_query,
    b_query,
    w_key,
    w_value,
    b_value,
    w_out,
    b_out,
):
    own = with_layout_constraint(frames[:, 0], Layout(major_to_minor=(0, 1, 2, 3)))
    frame_count, row_count, col_count, channels = own.shape
    inner = lax.axis_size("inner")
    bands = lax.axis_size("outer") * inner
    band = lax.axis_index("outer") * inner + lax.axis_index("inner")
    is_first = lax.axis_index("tm") == 0
    height = bands * row_count

    partner = lax.ppermute(own, "tm", [(0, 1), (1, 0)])
    even = jnp.where(is_first, own, partner)
    odd = jnp.where(is_first, partner, own)
    seq = jnp.stack([even, odd], axis=1).reshape(2 * frame_count, row_count, col_count, channels)

    up = [(2 * i, 2 * i + 2) for i in range(bands - 1)]
    down = [(2 * i + 3, 2 * i + 1) for i in range(bands - 1)]
    edge = jnp.where(is_first, seq[:, row_count - HALO :], seq[:, :HALO])
    arrived = lax.ppermute(edge, ("outer", "inner", "tm"), up + down)
    swapped = lax.ppermute(arrived, "tm", [(0, 1), (1, 0)])

    token_count = row_count * col_count
    residual, normed, folded = resnet_block(
        seq.reshape(2 * frame_count, -1, channels),
        arrived.reshape(2 * frame_count, -1, channels),
        swapped.reshape(2 * frame_count, -1, channels),
        norm1_gain,
        conv1_weight,
        conv1_bias,
        norm2_gain,
        conv2_weight,
        conv2_bias,
        attn_gain,
        w_query,
        b_query,
        w_key,
        col_count,
    )
    normed = normed.reshape(frame_count, row_count, col_count, channels)
    folded = folded.reshape(frame_count, token_count, channels)

    swap = [(0, 1), (1, 0)]
    partner_queries = lax.ppermute(folded, "inner", swap)
    keys = lax.all_gather(normed, "outer", axis=1, tiled=True)
    keys = keys.reshape(frame_count, -1, channels)
    def partial(queries):
        scores = jnp.einsum("fqc,fkc->fqk", queries, keys, preferred_element_type=jnp.float32)
        top = jnp.max(scores, axis=-1, keepdims=True)
        weights = jnp.exp(scores - top)
        total = jnp.sum(weights, axis=-1, keepdims=True)
        accum = jnp.einsum(
            "fqk,fkc->fqc", weights.astype(jnp.bfloat16), keys, preferred_element_type=jnp.float32
        )
        return accum, jnp.concatenate([top, total], axis=-1)

    back_accum, back_stats = partial(partner_queries)
    parts = []
    rest = back_stats
    for _ in range(3):
        head = lax.reduce_precision(rest, exponent_bits=8, mantissa_bits=7)
        parts.append(head)
        rest = rest - head
    packed = jnp.concatenate([back_accum] + parts, axis=-1).astype(jnp.bfloat16)
    returned = lax.ppermute(packed, "inner", swap).astype(jnp.float32)
    returned_accum = returned[..., :channels]
    pieces = [returned[..., channels + 2 * i : channels + 2 * i + 2] for i in range(3)]
    returned_stats = pieces[0] + (pieces[1] + pieces[2])
    mine_accum, mine_stats = partial(folded)
    top_mine = mine_stats[..., :1]
    top_back = returned_stats[..., :1]
    highest = jnp.maximum(top_mine, top_back)
    scale_mine = jnp.exp(top_mine - highest)
    scale_back = jnp.exp(top_back - highest)
    total = mine_stats[..., 1:] * scale_mine + returned_stats[..., 1:] * scale_back
    accum = mine_accum * scale_mine + returned_accum * scale_back
    mixed = (accum / total).astype(jnp.bfloat16).reshape(-1, channels)
    value = (jnp.dot(mixed, w_value, preferred_element_type=jnp.float32) + b_value).astype(
        jnp.bfloat16
    )
    decoded = (
        residual.reshape(-1, channels)
        + jnp.dot(value, w_out, preferred_element_type=jnp.float32)
        + b_out
    )
    return decoded.reshape(frame_count, 1, row_count, col_count, channels)


def solution(mesh):
    clips, bands, cores = mesh.devices.shape
    split = jax.sharding.Mesh(
        mesh.devices.reshape(clips, bands // 2, 2, cores), ("clips", "outer", "inner", "tm")
    )
    banded = P("clips", "tm", ("outer", "inner"), None, None)
    placed = (banded,) + (P(),) * 14
    return jax.shard_map(
        local,
        mesh=split,
        in_specs=placed,
        out_specs=banded,
        check_vma=False,
    )
```

```python
import functools
import math

import jax
import jax.numpy as jnp
from jax import lax
from jax.experimental import pallas as pl
from jax.experimental.layout import Layout, with_layout_constraint
from jax.experimental.pallas import tpu as pltpu
from jax.sharding import PartitionSpec as P

epsilon = 1e-06
HALO = 2


def rms_scale(values, gain):
    return values * lax.rsqrt(jnp.mean(values * values, axis=-1, keepdims=True) + epsilon) * gain


def conv_rows(source, taps):
    return lax.conv_general_dilated(
        source,
        taps,
        window_strides=(1, 1),
        padding=((0, 0), (1, 1)),
        dimension_numbers=("NHWC", "HWIO", "NHWC"),
        preferred_element_type=jnp.float32,
    )


def causal_time_conv(seq, weight):
    frame_total = seq.shape[0]
    out = None
    for p in range(3):
        lag = 2 - p
        if lag >= frame_total:
            continue
        part = conv_rows(seq[: frame_total - lag], weight[p])
        if lag:
            part = jnp.pad(part, ((lag, 0), (0, 0), (0, 0), (0, 0)))
        out = part if out is None else out + part
    return out


def _rms(v, g):
    return v * lax.rsqrt(jnp.mean(v * v, axis=-1, keepdims=True) + epsilon) * g

def _silu(v):
    return v * (1.0 / (1.0 + jnp.exp(-v)))

def block_kernel(cols, frame_count, seq_ref, arrived_ref, swapped_ref, g1_ref, w1_ref, b1_ref, g2_ref,
                 w2_ref, b2_ref, ga_ref, wq_ref, bq_ref, wk_ref, res_ref, normed_ref, folded_ref):
    total = 2 * frame_count
    p_out = seq_ref.shape[1]
    p_mid = p_out + 2 * cols
    first = lax.axis_index("tm") == 0

    def extended(t):
        above = jnp.where(first, arrived_ref[t], swapped_ref[t])
        below = jnp.where(first, swapped_ref[t], arrived_ref[t])
        return jnp.concatenate([above, seq_ref[t], below], axis=0)

    def shifted(a):
        n = a.shape[0]
        col = lax.broadcasted_iota(jnp.int32, (n, 1), 0) % cols
        left = jnp.where(col == 0, 0.0, pltpu.roll(a, 1, 0))
        right = jnp.where(col == cols - 1, 0.0, pltpu.roll(a, n - 1, 0))
        return [left.astype(jnp.bfloat16), a.astype(jnp.bfloat16), right.astype(jnp.bfloat16)]

    def conv_frame(sources, w_ref, out_rows):
        acc = None
        for p, trip in enumerate(sources):
            if trip is None:
                continue
            for q in range(3):
                for s in range(3):
                    window = trip[s][q * cols: q * cols + out_rows]
                    part = jnp.dot(window, w_ref[(p * 3 + q) * 3 + s], preferred_element_type=jnp.float32)
                    acc = part if acc is None else acc + part
        return acc

    g1 = g1_ref[...]
    act1 = [shifted(_silu(_rms(extended(t).astype(jnp.float32), g1)).astype(jnp.bfloat16).astype(jnp.float32)) for t in range(total)]
    inner = lax.axis_size("inner")
    band = lax.axis_index("outer") * inner + lax.axis_index("inner")
    band_rows = p_out // cols
    height = lax.axis_size("outer") * inner * band_rows
    lo = 1 - band * band_rows
    hi = height - band * band_rows + 1
    row = lax.broadcasted_iota(jnp.int32, (p_mid, 1), 0) // cols
    inside = (row >= lo) & (row < hi)
    g2 = g2_ref[...]
    b1 = b1_ref[...]
    act2 = []
    for j in range(total):
        srcs = [act1[j + p - 2] if j + p - 2 >= 0 else None for p in range(3)]
        out1 = conv_frame(srcs, w1_ref, p_mid) + b1
        act2.append(jnp.where(inside, _silu(_rms(out1, g2)), 0.0).astype(jnp.bfloat16).astype(jnp.float32))
    b2 = b2_ref[...]
    ga = ga_ref[...]
    zero = None
    for k in range(frame_count):
        def pick(t_even):
            a = act2[t_even] if 0 <= t_even < total else None
            b = act2[t_even + 1] if 0 <= t_even + 1 < total else None
            if a is None and b is None:
                return None
            a = jnp.zeros_like(act2[0]) if a is None else a
            b = jnp.zeros_like(act2[0]) if b is None else b
            return shifted(jnp.where(first, a, b))
        srcs = [pick(2 * k - 2), pick(2 * k - 1), pick(2 * k)]
        out2 = conv_frame(srcs, w2_ref, p_out) + b2
        own = jnp.where(first, seq_ref[2 * k], seq_ref[2 * k + 1])
        res = own.astype(jnp.float32) + out2
        res_ref[k] = res
        normed = _rms(res, ga).astype(jnp.bfloat16)
        normed_ref[k] = normed
        query = jnp.dot(normed, wq_ref[...], preferred_element_type=jnp.float32) + bq_ref[...]
        folded = lax.dot_general(
            query.astype(jnp.bfloat16), wk_ref[...], (((1,), (1,)), ((), ())),
            preferred_element_type=jnp.float32,
        )
        folded_ref[k] = (folded * (1.0 / math.sqrt(res.shape[-1]))).astype(jnp.bfloat16)

def resnet_block(seq, arrived, swapped, g1, w1, b1, g2, w2, b2, ga, wq, bq, wk, cols):
    total, p_out, c = seq.shape
    frame_count = total // 2
    vm = pl.BlockSpec(memory_space=pltpu.VMEM)
    return pl.pallas_call(
        functools.partial(block_kernel, cols, frame_count),
        out_shape=(jax.ShapeDtypeStruct((frame_count, p_out, c), jnp.float32),
                   jax.ShapeDtypeStruct((frame_count, p_out, c), jnp.bfloat16),
                   jax.ShapeDtypeStruct((frame_count, p_out, c), jnp.bfloat16)),
        in_specs=[vm] * 13,
        out_specs=(vm, vm, vm),
    )(seq, arrived, swapped, g1.reshape(1, c), w1.reshape(27, c, c), b1.reshape(1, c), g2.reshape(1, c),
      w2.reshape(27, c, c), b2.reshape(1, c), ga.reshape(1, c), wq, bq.reshape(1, c), wk)


def local(
    frames,
    norm1_gain,
    conv1_weight,
    conv1_bias,
    norm2_gain,
    conv2_weight,
    conv2_bias,
    attn_gain,
    w_query,
    b_query,
    w_key,
    w_value,
    b_value,
    w_out,
    b_out,
):
    own = with_layout_constraint(frames[:, 0], Layout(major_to_minor=(0, 1, 2, 3)))
    frame_count, row_count, col_count, channels = own.shape
    inner = lax.axis_size("inner")
    bands = lax.axis_size("outer") * inner
    band = lax.axis_index("outer") * inner + lax.axis_index("inner")
    is_first = lax.axis_index("tm") == 0
    height = bands * row_count

    partner = lax.ppermute(own, "tm", [(0, 1), (1, 0)])
    even = jnp.where(is_first, own, partner)
    odd = jnp.where(is_first, partner, own)
    seq = jnp.stack([even, odd], axis=1).reshape(2 * frame_count, row_count, col_count, channels)

    up = [(2 * i, 2 * i + 2) for i in range(bands - 1)]
    down = [(2 * i + 3, 2 * i + 1) for i in range(bands - 1)]
    edge = jnp.where(is_first, seq[:, row_count - HALO :], seq[:, :HALO])
    arrived = lax.ppermute(edge, ("outer", "inner", "tm"), up + down)
    swapped = lax.ppermute(arrived, "tm", [(0, 1), (1, 0)])

    token_count = row_count * col_count
    residual, normed, folded = resnet_block(
        seq.reshape(2 * frame_count, -1, channels),
        arrived.reshape(2 * frame_count, -1, channels),
        swapped.reshape(2 * frame_count, -1, channels),
        norm1_gain,
        conv1_weight,
        conv1_bias,
        norm2_gain,
        conv2_weight,
        conv2_bias,
        attn_gain,
        w_query,
        b_query,
        w_key,
        col_count,
    )
    normed = normed.reshape(frame_count, row_count, col_count, channels)
    folded = folded.reshape(frame_count, token_count, channels)

    swap = [(0, 1), (1, 0)]
    partner_queries = lax.ppermute(folded, "inner", swap)
    spans = lax.axis_size("outer")
    if spans <= 4:
        shares = [normed] + [
            lax.ppermute(normed, "outer", [(i, (i + k) % spans) for i in range(spans)])
            for k in range(1, spans)
        ]
        keys = jnp.concatenate(shares, axis=1)
    else:
        keys = lax.all_gather(normed, "outer", axis=1, tiled=True)
    keys = keys.reshape(frame_count, -1, channels)
    def partial(queries):
        scores = jnp.einsum("fqc,fkc->fqk", queries, keys, preferred_element_type=jnp.float32)
        top = jnp.max(scores, axis=-1, keepdims=True)
        weights = jnp.exp(scores - top)
        total = jnp.sum(weights, axis=-1, keepdims=True)
        accum = jnp.einsum(
            "fqk,fkc->fqc", weights.astype(jnp.bfloat16), keys, preferred_element_type=jnp.float32
        )
        return accum, jnp.concatenate([top, total], axis=-1)

    back_accum, back_stats = partial(partner_queries)
    returned_accum, returned_stats = lax.ppermute(
        (back_accum.astype(jnp.bfloat16), back_stats), "inner", swap
    )
    mine_accum, mine_stats = partial(folded)
    top_mine = mine_stats[..., :1]
    top_back = returned_stats[..., :1]
    highest = jnp.maximum(top_mine, top_back)
    scale_mine = jnp.exp(top_mine - highest)
    scale_back = jnp.exp(top_back - highest)
    total = mine_stats[..., 1:] * scale_mine + returned_stats[..., 1:] * scale_back
    accum = mine_accum * scale_mine + returned_accum.astype(jnp.float32) * scale_back
    mixed = (accum / total).astype(jnp.bfloat16).reshape(-1, channels)
    value = (jnp.dot(mixed, w_value, preferred_element_type=jnp.float32) + b_value).astype(
        jnp.bfloat16
    )
    decoded = (
        residual.reshape(-1, channels)
        + jnp.dot(value, w_out, preferred_element_type=jnp.float32)
        + b_out
    )
    return decoded.reshape(frame_count, 1, row_count, col_count, channels)


def solution(mesh):
    clips, bands, cores = mesh.devices.shape
    split = jax.sharding.Mesh(
        mesh.devices.reshape(clips, bands // 2, 2, cores), ("clips", "outer", "inner", "tm")
    )
    banded = P("clips", "tm", ("outer", "inner"), None, None)
    placed = (banded,) + (P(),) * 14
    return jax.shard_map(
        local,
        mesh=split,
        in_specs=placed,
        out_specs=banded,
        check_vma=False,
    )
```

```python
import functools
import math

import jax
import jax.numpy as jnp
from jax import lax
from jax.experimental import pallas as pl
from jax.experimental.layout import Layout, with_layout_constraint
from jax.experimental.pallas import tpu as pltpu
from jax.sharding import PartitionSpec as P

epsilon = 1e-06
HALO = 2


def rms_scale(values, gain):
    return values * lax.rsqrt(jnp.mean(values * values, axis=-1, keepdims=True) + epsilon) * gain


def conv_rows(source, taps):
    return lax.conv_general_dilated(
        source,
        taps,
        window_strides=(1, 1),
        padding=((0, 0), (1, 1)),
        dimension_numbers=("NHWC", "HWIO", "NHWC"),
        preferred_element_type=jnp.float32,
    )


def causal_time_conv(seq, weight):
    frame_total = seq.shape[0]
    out = None
    for p in range(3):
        lag = 2 - p
        if lag >= frame_total:
            continue
        part = conv_rows(seq[: frame_total - lag], weight[p])
        if lag:
            part = jnp.pad(part, ((lag, 0), (0, 0), (0, 0), (0, 0)))
        out = part if out is None else out + part
    return out


def _rms(v, g):
    return v * lax.rsqrt(jnp.mean(v * v, axis=-1, keepdims=True) + epsilon) * g

def _silu(v):
    return v * (1.0 / (1.0 + jnp.exp(-v)))

def block_kernel(cols, frame_count, seq_ref, arrived_ref, swapped_ref, g1_ref, w1_ref, b1_ref, g2_ref,
                 w2_ref, b2_ref, ga_ref, wq_ref, bq_ref, wk_ref, res_ref, normed_ref, folded_ref):
    total = 2 * frame_count
    p_out = seq_ref.shape[1]
    p_mid = p_out + 2 * cols
    first = lax.axis_index("tm") == 0

    def extended(t):
        above = jnp.where(first, arrived_ref[t], swapped_ref[t])
        below = jnp.where(first, swapped_ref[t], arrived_ref[t])
        return jnp.concatenate([above, seq_ref[t], below], axis=0)

    def shifted(a):
        n = a.shape[0]
        col = lax.broadcasted_iota(jnp.int32, (n, 1), 0) % cols
        left = jnp.where(col == 0, 0.0, pltpu.roll(a, 1, 0))
        right = jnp.where(col == cols - 1, 0.0, pltpu.roll(a, n - 1, 0))
        return [left.astype(jnp.bfloat16), a.astype(jnp.bfloat16), right.astype(jnp.bfloat16)]

    def conv_frame(sources, w_ref, out_rows):
        acc = None
        for p, trip in enumerate(sources):
            if trip is None:
                continue
            for q in range(3):
                for s in range(3):
                    window = trip[s][q * cols: q * cols + out_rows]
                    part = jnp.dot(window, w_ref[(p * 3 + q) * 3 + s], preferred_element_type=jnp.float32)
                    acc = part if acc is None else acc + part
        return acc

    g1 = g1_ref[...]
    act1 = [shifted(_silu(_rms(extended(t).astype(jnp.float32), g1)).astype(jnp.bfloat16).astype(jnp.float32)) for t in range(total)]
    inner = lax.axis_size("inner")
    band = lax.axis_index("outer") * inner + lax.axis_index("inner")
    band_rows = p_out // cols
    height = lax.axis_size("outer") * inner * band_rows
    lo = 1 - band * band_rows
    hi = height - band * band_rows + 1
    row = lax.broadcasted_iota(jnp.int32, (p_mid, 1), 0) // cols
    inside = (row >= lo) & (row < hi)
    g2 = g2_ref[...]
    b1 = b1_ref[...]
    act2 = []
    for j in range(total):
        srcs = [act1[j + p - 2] if j + p - 2 >= 0 else None for p in range(3)]
        out1 = conv_frame(srcs, w1_ref, p_mid) + b1
        act2.append(jnp.where(inside, _silu(_rms(out1, g2)), 0.0).astype(jnp.bfloat16).astype(jnp.float32))
    b2 = b2_ref[...]
    ga = ga_ref[...]
    zero = None
    for k in range(frame_count):
        def pick(t_even):
            a = act2[t_even] if 0 <= t_even < total else None
            b = act2[t_even + 1] if 0 <= t_even + 1 < total else None
            if a is None and b is None:
                return None
            a = jnp.zeros_like(act2[0]) if a is None else a
            b = jnp.zeros_like(act2[0]) if b is None else b
            return shifted(jnp.where(first, a, b))
        srcs = [pick(2 * k - 2), pick(2 * k - 1), pick(2 * k)]
        out2 = conv_frame(srcs, w2_ref, p_out) + b2
        own = jnp.where(first, seq_ref[2 * k], seq_ref[2 * k + 1])
        res = own.astype(jnp.float32) + out2
        res_ref[k] = res
        normed = _rms(res, ga).astype(jnp.bfloat16)
        normed_ref[k] = normed
        query = jnp.dot(normed, wq_ref[...], preferred_element_type=jnp.float32) + bq_ref[...]
        folded = lax.dot_general(
            query.astype(jnp.bfloat16), wk_ref[...], (((1,), (1,)), ((), ())),
            preferred_element_type=jnp.float32,
        )
        folded_ref[k] = (folded * (1.0 / math.sqrt(res.shape[-1]))).astype(jnp.bfloat16)

def resnet_block(seq, arrived, swapped, g1, w1, b1, g2, w2, b2, ga, wq, bq, wk, cols):
    total, p_out, c = seq.shape
    frame_count = total // 2
    vm = pl.BlockSpec(memory_space=pltpu.VMEM)
    return pl.pallas_call(
        functools.partial(block_kernel, cols, frame_count),
        out_shape=(jax.ShapeDtypeStruct((frame_count, p_out, c), jnp.float32),
                   jax.ShapeDtypeStruct((frame_count, p_out, c), jnp.bfloat16),
                   jax.ShapeDtypeStruct((frame_count, p_out, c), jnp.bfloat16)),
        in_specs=[vm] * 13,
        out_specs=(vm, vm, vm),
    )(seq, arrived, swapped, g1.reshape(1, c), w1.reshape(27, c, c), b1.reshape(1, c), g2.reshape(1, c),
      w2.reshape(27, c, c), b2.reshape(1, c), ga.reshape(1, c), wq, bq.reshape(1, c), wk)


def local(
    frames,
    norm1_gain,
    conv1_weight,
    conv1_bias,
    norm2_gain,
    conv2_weight,
    conv2_bias,
    attn_gain,
    w_query,
    b_query,
    w_key,
    w_value,
    b_value,
    w_out,
    b_out,
):
    own = with_layout_constraint(frames[:, 0], Layout(major_to_minor=(0, 1, 2, 3)))
    frame_count, row_count, col_count, channels = own.shape
    inner = lax.axis_size("inner")
    bands = lax.axis_size("outer") * inner
    band = lax.axis_index("outer") * inner + lax.axis_index("inner")
    is_first = lax.axis_index("tm") == 0
    height = bands * row_count

    partner = lax.ppermute(own, "tm", [(0, 1), (1, 0)])
    even = jnp.where(is_first, own, partner)
    odd = jnp.where(is_first, partner, own)
    seq = jnp.stack([even, odd], axis=1).reshape(2 * frame_count, row_count, col_count, channels)

    up = [(2 * i, 2 * i + 2) for i in range(bands - 1)]
    down = [(2 * i + 3, 2 * i + 1) for i in range(bands - 1)]
    edge = jnp.where(is_first, seq[:, row_count - HALO :], seq[:, :HALO])
    arrived = lax.ppermute(edge, ("outer", "inner", "tm"), up + down)
    swapped = lax.ppermute(arrived, "tm", [(0, 1), (1, 0)])

    token_count = row_count * col_count
    residual, normed, folded = resnet_block(
        seq.reshape(2 * frame_count, -1, channels),
        arrived.reshape(2 * frame_count, -1, channels),
        swapped.reshape(2 * frame_count, -1, channels),
        norm1_gain,
        conv1_weight,
        conv1_bias,
        norm2_gain,
        conv2_weight,
        conv2_bias,
        attn_gain,
        w_query,
        b_query,
        w_key,
        col_count,
    )
    normed = normed.reshape(frame_count, row_count, col_count, channels)
    folded = folded.reshape(frame_count, token_count, channels)

    swap = [(0, 1), (1, 0)]
    partner_queries = lax.ppermute(folded, "inner", swap)
    spans = lax.axis_size("outer")
    if spans <= 4:
        shares = [normed] + [
            lax.ppermute(normed, "outer", [(i, (i + k) % spans) for i in range(spans)])
            for k in range(1, spans)
        ]
        keys = jnp.concatenate(shares, axis=1)
    else:
        keys = lax.all_gather(normed, "outer", axis=1, tiled=True)
    keys = keys.reshape(frame_count, -1, channels)
    def partial(queries):
        scores = jnp.einsum("fqc,fkc->fqk", queries, keys, preferred_element_type=jnp.float32)
        top = jnp.max(scores, axis=-1, keepdims=True)
        weights = jnp.exp(scores - top)
        total = jnp.sum(weights, axis=-1, keepdims=True)
        accum = jnp.einsum(
            "fqk,fkc->fqc", weights.astype(jnp.bfloat16), keys, preferred_element_type=jnp.float32
        )
        return accum, jnp.concatenate([top, total], axis=-1)

    back_accum, back_stats = partial(partner_queries)
    parts = []
    rest = back_stats
    for _ in range(3):
        head = lax.reduce_precision(rest, exponent_bits=8, mantissa_bits=7)
        parts.append(head)
        rest = rest - head
    packed = jnp.concatenate([back_accum] + parts, axis=-1).astype(jnp.bfloat16)
    returned = lax.ppermute(packed, "inner", swap).astype(jnp.float32)
    returned_accum = returned[..., :channels]
    pieces = [returned[..., channels + 2 * i : channels + 2 * i + 2] for i in range(3)]
    returned_stats = pieces[0] + (pieces[1] + pieces[2])
    mine_accum, mine_stats = partial(folded)
    top_mine = mine_stats[..., :1]
    top_back = returned_stats[..., :1]
    highest = jnp.maximum(top_mine, top_back)
    scale_mine = jnp.exp(top_mine - highest)
    scale_back = jnp.exp(top_back - highest)
    total = mine_stats[..., 1:] * scale_mine + returned_stats[..., 1:] * scale_back
    accum = mine_accum * scale_mine + returned_accum * scale_back
    mixed = (accum / total).astype(jnp.bfloat16).reshape(-1, channels)
    value = (jnp.dot(mixed, w_value, preferred_element_type=jnp.float32) + b_value).astype(
        jnp.bfloat16
    )
    decoded = (
        residual.reshape(-1, channels)
        + jnp.dot(value, w_out, preferred_element_type=jnp.float32)
        + b_out
    )
    return decoded.reshape(frame_count, 1, row_count, col_count, channels)


def solution(mesh):
    clips, bands, cores = mesh.devices.shape
    split = jax.sharding.Mesh(
        mesh.devices.reshape(clips, bands // 2, 2, cores), ("clips", "outer", "inner", "tm")
    )
    banded = P("clips", "tm", ("outer", "inner"), None, None)
    placed = (banded,) + (P(),) * 14
    return jax.shard_map(
        local,
        mesh=split,
        in_specs=placed,
        out_specs=banded,
        check_vma=False,
    )
```

```python
import functools
import math

import jax
import jax.numpy as jnp
from jax import lax
from jax.experimental import pallas as pl
from jax.experimental.layout import Layout, with_layout_constraint
from jax.experimental.pallas import tpu as pltpu
from jax.sharding import PartitionSpec as P

epsilon = 1e-06
HALO = 2


def rms_scale(values, gain):
    return values * lax.rsqrt(jnp.mean(values * values, axis=-1, keepdims=True) + epsilon) * gain


def conv_rows(source, taps):
    return lax.conv_general_dilated(
        source,
        taps,
        window_strides=(1, 1),
        padding=((0, 0), (1, 1)),
        dimension_numbers=("NHWC", "HWIO", "NHWC"),
        preferred_element_type=jnp.float32,
    )


def causal_time_conv(seq, weight):
    frame_total = seq.shape[0]
    out = None
    for p in range(3):
        lag = 2 - p
        if lag >= frame_total:
            continue
        part = conv_rows(seq[: frame_total - lag], weight[p])
        if lag:
            part = jnp.pad(part, ((lag, 0), (0, 0), (0, 0), (0, 0)))
        out = part if out is None else out + part
    return out


def _rms(v, g):
    return v * lax.rsqrt(jnp.mean(v * v, axis=-1, keepdims=True) + epsilon) * g

def _silu(v):
    return v * (1.0 / (1.0 + jnp.exp(-v)))

def block_kernel(cols, frame_count, seq_ref, arrived_ref, swapped_ref, g1_ref, w1_ref, b1_ref, g2_ref,
                 w2_ref, b2_ref, ga_ref, wq_ref, bq_ref, wk_ref, res_ref, normed_ref, folded_ref):
    total = 2 * frame_count
    p_out = seq_ref.shape[1]
    p_mid = p_out + 2 * cols
    first = lax.axis_index("tm") == 0

    def extended(t):
        above = jnp.where(first, arrived_ref[t], swapped_ref[t])
        below = jnp.where(first, swapped_ref[t], arrived_ref[t])
        return jnp.concatenate([above, seq_ref[t], below], axis=0)

    def shifted(a):
        n = a.shape[0]
        col = lax.broadcasted_iota(jnp.int32, (n, 1), 0) % cols
        left = jnp.where(col == 0, 0.0, pltpu.roll(a, 1, 0))
        right = jnp.where(col == cols - 1, 0.0, pltpu.roll(a, n - 1, 0))
        return [left.astype(jnp.bfloat16), a.astype(jnp.bfloat16), right.astype(jnp.bfloat16)]

    def conv_frame(sources, w_ref, out_rows):
        acc = None
        for p, trip in enumerate(sources):
            if trip is None:
                continue
            for q in range(3):
                for s in range(3):
                    window = trip[s][q * cols: q * cols + out_rows]
                    part = jnp.dot(window, w_ref[(p * 3 + q) * 3 + s], preferred_element_type=jnp.float32)
                    acc = part if acc is None else acc + part
        return acc

    g1 = g1_ref[...]
    act1 = [shifted(_silu(_rms(extended(t).astype(jnp.float32), g1)).astype(jnp.bfloat16).astype(jnp.float32)) for t in range(total)]
    inner = lax.axis_size("inner")
    band = lax.axis_index("outer") * inner + lax.axis_index("inner")
    band_rows = p_out // cols
    height = lax.axis_size("outer") * inner * band_rows
    lo = 1 - band * band_rows
    hi = height - band * band_rows + 1
    row = lax.broadcasted_iota(jnp.int32, (p_mid, 1), 0) // cols
    inside = (row >= lo) & (row < hi)
    g2 = g2_ref[...]
    b1 = b1_ref[...]
    act2 = []
    for j in range(total):
        srcs = [act1[j + p - 2] if j + p - 2 >= 0 else None for p in range(3)]
        out1 = conv_frame(srcs, w1_ref, p_mid) + b1
        act2.append(jnp.where(inside, _silu(_rms(out1, g2)), 0.0).astype(jnp.bfloat16).astype(jnp.float32))
    b2 = b2_ref[...]
    ga = ga_ref[...]
    zero = None
    for k in range(frame_count):
        def pick(t_even):
            a = act2[t_even] if 0 <= t_even < total else None
            b = act2[t_even + 1] if 0 <= t_even + 1 < total else None
            if a is None and b is None:
                return None
            a = jnp.zeros_like(act2[0]) if a is None else a
            b = jnp.zeros_like(act2[0]) if b is None else b
            return shifted(jnp.where(first, a, b))
        srcs = [pick(2 * k - 2), pick(2 * k - 1), pick(2 * k)]
        out2 = conv_frame(srcs, w2_ref, p_out) + b2
        own = jnp.where(first, seq_ref[2 * k], seq_ref[2 * k + 1])
        res = own.astype(jnp.float32) + out2
        res_ref[k] = res
        normed = _rms(res, ga).astype(jnp.bfloat16)
        normed_ref[k] = normed
        query = jnp.dot(normed, wq_ref[...], preferred_element_type=jnp.float32) + bq_ref[...]
        folded = lax.dot_general(
            query.astype(jnp.bfloat16), wk_ref[...], (((1,), (1,)), ((), ())),
            preferred_element_type=jnp.float32,
        )
        folded_ref[k] = (folded * (1.0 / math.sqrt(res.shape[-1]))).astype(jnp.bfloat16)

def resnet_block(seq, arrived, swapped, g1, w1, b1, g2, w2, b2, ga, wq, bq, wk, cols):
    total, p_out, c = seq.shape
    frame_count = total // 2
    vm = pl.BlockSpec(memory_space=pltpu.VMEM)
    return pl.pallas_call(
        functools.partial(block_kernel, cols, frame_count),
        out_shape=(jax.ShapeDtypeStruct((frame_count, p_out, c), jnp.float32),
                   jax.ShapeDtypeStruct((frame_count, p_out, c), jnp.bfloat16),
                   jax.ShapeDtypeStruct((frame_count, p_out, c), jnp.bfloat16)),
        in_specs=[vm] * 13,
        out_specs=(vm, vm, vm),
    )(seq, arrived, swapped, g1.reshape(1, c), w1.reshape(27, c, c), b1.reshape(1, c), g2.reshape(1, c),
      w2.reshape(27, c, c), b2.reshape(1, c), ga.reshape(1, c), wq, bq.reshape(1, c), wk)


def local(
    frames,
    norm1_gain,
    conv1_weight,
    conv1_bias,
    norm2_gain,
    conv2_weight,
    conv2_bias,
    attn_gain,
    w_query,
    b_query,
    w_key,
    w_value,
    b_value,
    w_out,
    b_out,
):
    own = with_layout_constraint(frames[:, 0], Layout(major_to_minor=(0, 1, 2, 3)))
    frame_count, row_count, col_count, channels = own.shape
    inner = lax.axis_size("inner")
    bands = lax.axis_size("outer") * inner
    band = lax.axis_index("outer") * inner + lax.axis_index("inner")
    is_first = lax.axis_index("tm") == 0
    height = bands * row_count

    partner = lax.ppermute(own, "tm", [(0, 1), (1, 0)])
    even = jnp.where(is_first, own, partner)
    odd = jnp.where(is_first, partner, own)
    seq = jnp.stack([even, odd], axis=1).reshape(2 * frame_count, row_count, col_count, channels)

    up = [(2 * i, 2 * i + 2) for i in range(bands - 1)]
    down = [(2 * i + 3, 2 * i + 1) for i in range(bands - 1)]
    edge = jnp.where(is_first, seq[:, row_count - HALO :], seq[:, :HALO])
    arrived = lax.ppermute(edge, ("outer", "inner", "tm"), up + down)
    swapped = lax.ppermute(arrived, "tm", [(0, 1), (1, 0)])

    token_count = row_count * col_count
    residual, normed, folded = resnet_block(
        seq.reshape(2 * frame_count, -1, channels),
        arrived.reshape(2 * frame_count, -1, channels),
        swapped.reshape(2 * frame_count, -1, channels),
        norm1_gain,
        conv1_weight,
        conv1_bias,
        norm2_gain,
        conv2_weight,
        conv2_bias,
        attn_gain,
        w_query,
        b_query,
        w_key,
        col_count,
    )
    normed = normed.reshape(frame_count, row_count, col_count, channels)
    folded = folded.reshape(frame_count, token_count, channels)

    swap = [(0, 1), (1, 0)]
    partner_queries = lax.ppermute(folded, "inner", swap)
    spans = lax.axis_size("outer")
    if spans <= 4:
        if spans & (spans - 1) == 0:
            routes = [[(i, i ^ k) for i in range(spans)] for k in range(1, spans)]
        else:
            routes = [[(i, (i + k) % spans) for i in range(spans)] for k in range(1, spans)]
        shares = [normed] + [lax.ppermute(normed, "outer", route) for route in routes]
        keys = jnp.concatenate(shares, axis=1)
    else:
        keys = lax.all_gather(normed, "outer", axis=1, tiled=True)
    keys = keys.reshape(frame_count, -1, channels)
    def partial(queries):
        scores = jnp.einsum("fqc,fkc->fqk", queries, keys, preferred_element_type=jnp.float32)
        top = jnp.max(scores, axis=-1, keepdims=True)
        weights = jnp.exp(scores - top)
        total = jnp.sum(weights, axis=-1, keepdims=True)
        accum = jnp.einsum(
            "fqk,fkc->fqc", weights.astype(jnp.bfloat16), keys, preferred_element_type=jnp.float32
        )
        return accum, jnp.concatenate([top, total], axis=-1)

    back_accum, back_stats = partial(partner_queries)
    parts = []
    rest = back_stats
    for _ in range(3):
        head = lax.reduce_precision(rest, exponent_bits=8, mantissa_bits=7)
        parts.append(head)
        rest = rest - head
    packed = jnp.concatenate([back_accum] + parts, axis=-1).astype(jnp.bfloat16)
    returned = lax.ppermute(packed, "inner", swap).astype(jnp.float32)
    returned_accum = returned[..., :channels]
    pieces = [returned[..., channels + 2 * i : channels + 2 * i + 2] for i in range(3)]
    returned_stats = pieces[0] + (pieces[1] + pieces[2])
    mine_accum, mine_stats = partial(folded)
    top_mine = mine_stats[..., :1]
    top_back = returned_stats[..., :1]
    highest = jnp.maximum(top_mine, top_back)
    scale_mine = jnp.exp(top_mine - highest)
    scale_back = jnp.exp(top_back - highest)
    total = mine_stats[..., 1:] * scale_mine + returned_stats[..., 1:] * scale_back
    accum = mine_accum * scale_mine + returned_accum * scale_back
    mixed = (accum / total).astype(jnp.bfloat16).reshape(-1, channels)
    value = (jnp.dot(mixed, w_value, preferred_element_type=jnp.float32) + b_value).astype(
        jnp.bfloat16
    )
    decoded = (
        residual.reshape(-1, channels)
        + jnp.dot(value, w_out, preferred_element_type=jnp.float32)
        + b_out
    )
    return decoded.reshape(frame_count, 1, row_count, col_count, channels)


def solution(mesh):
    clips, bands, cores = mesh.devices.shape
    split = jax.sharding.Mesh(
        mesh.devices.reshape(clips, bands // 2, 2, cores), ("clips", "outer", "inner", "tm")
    )
    banded = P("clips", "tm", ("outer", "inner"), None, None)
    placed = (banded,) + (P(),) * 14
    return jax.shard_map(
        local,
        mesh=split,
        in_specs=placed,
        out_specs=banded,
        check_vma=False,
    )
```

```python
import functools
import math

import jax
import jax.numpy as jnp
from jax import lax
from jax.experimental import pallas as pl
from jax.experimental.layout import Layout, with_layout_constraint
from jax.experimental.pallas import tpu as pltpu
from jax.sharding import PartitionSpec as P

epsilon = 1e-06
HALO = 2


def rms_scale(values, gain):
    return values * lax.rsqrt(jnp.mean(values * values, axis=-1, keepdims=True) + epsilon) * gain


def conv_rows(source, taps):
    return lax.conv_general_dilated(
        source,
        taps,
        window_strides=(1, 1),
        padding=((0, 0), (1, 1)),
        dimension_numbers=("NHWC", "HWIO", "NHWC"),
        preferred_element_type=jnp.float32,
    )


def causal_time_conv(seq, weight):
    frame_total = seq.shape[0]
    out = None
    for p in range(3):
        lag = 2 - p
        if lag >= frame_total:
            continue
        part = conv_rows(seq[: frame_total - lag], weight[p])
        if lag:
            part = jnp.pad(part, ((lag, 0), (0, 0), (0, 0), (0, 0)))
        out = part if out is None else out + part
    return out


def _rms(v, g):
    return v * lax.rsqrt(jnp.mean(v * v, axis=-1, keepdims=True) + epsilon) * g

def _silu(v):
    return v * (1.0 / (1.0 + jnp.exp(-v)))

def block_kernel(cols, frame_count, seq_ref, arrived_ref, swapped_ref, g1_ref, w1_ref, b1_ref, g2_ref,
                 w2_ref, b2_ref, ga_ref, wq_ref, bq_ref, wk_ref, res_ref, normed_ref, folded_ref):
    total = 2 * frame_count
    p_out = seq_ref.shape[1]
    p_mid = p_out + 2 * cols
    first = lax.axis_index("tm") == 0

    def extended(t):
        above = jnp.where(first, arrived_ref[t], swapped_ref[t])
        below = jnp.where(first, swapped_ref[t], arrived_ref[t])
        return jnp.concatenate([above, seq_ref[t], below], axis=0)

    def shifted(a):
        n = a.shape[0]
        col = lax.broadcasted_iota(jnp.int32, (n, 1), 0) % cols
        left = jnp.where(col == 0, 0.0, pltpu.roll(a, 1, 0))
        right = jnp.where(col == cols - 1, 0.0, pltpu.roll(a, n - 1, 0))
        return [left.astype(jnp.bfloat16), a.astype(jnp.bfloat16), right.astype(jnp.bfloat16)]

    def conv_frame(sources, w_ref, out_rows):
        acc = None
        for p, trip in enumerate(sources):
            if trip is None:
                continue
            for q in range(3):
                for s in range(3):
                    window = trip[s][q * cols: q * cols + out_rows]
                    part = jnp.dot(window, w_ref[(p * 3 + q) * 3 + s], preferred_element_type=jnp.float32)
                    acc = part if acc is None else acc + part
        return acc

    g1 = g1_ref[...]
    act1 = [shifted(_silu(_rms(extended(t).astype(jnp.float32), g1)).astype(jnp.bfloat16).astype(jnp.float32)) for t in range(total)]
    inner = lax.axis_size("inner")
    band = lax.axis_index("outer") * inner + lax.axis_index("inner")
    band_rows = p_out // cols
    height = lax.axis_size("outer") * inner * band_rows
    lo = 1 - band * band_rows
    hi = height - band * band_rows + 1
    row = lax.broadcasted_iota(jnp.int32, (p_mid, 1), 0) // cols
    inside = (row >= lo) & (row < hi)
    g2 = g2_ref[...]
    b1 = b1_ref[...]
    act2 = []
    for j in range(total):
        srcs = [act1[j + p - 2] if j + p - 2 >= 0 else None for p in range(3)]
        out1 = conv_frame(srcs, w1_ref, p_mid) + b1
        act2.append(jnp.where(inside, _silu(_rms(out1, g2)), 0.0).astype(jnp.bfloat16).astype(jnp.float32))
    b2 = b2_ref[...]
    ga = ga_ref[...]
    zero = None
    for k in range(frame_count):
        def pick(t_even):
            a = act2[t_even] if 0 <= t_even < total else None
            b = act2[t_even + 1] if 0 <= t_even + 1 < total else None
            if a is None and b is None:
                return None
            a = jnp.zeros_like(act2[0]) if a is None else a
            b = jnp.zeros_like(act2[0]) if b is None else b
            return shifted(jnp.where(first, a, b))
        srcs = [pick(2 * k - 2), pick(2 * k - 1), pick(2 * k)]
        out2 = conv_frame(srcs, w2_ref, p_out) + b2
        own = jnp.where(first, seq_ref[2 * k], seq_ref[2 * k + 1])
        res = own.astype(jnp.float32) + out2
        res_ref[k] = res
        normed = _rms(res, ga).astype(jnp.bfloat16)
        normed_ref[k] = normed
        query = jnp.dot(normed, wq_ref[...], preferred_element_type=jnp.float32) + bq_ref[...]
        folded = lax.dot_general(
            query.astype(jnp.bfloat16), wk_ref[...], (((1,), (1,)), ((), ())),
            preferred_element_type=jnp.float32,
        )
        folded_ref[k] = (folded * (1.0 / math.sqrt(res.shape[-1]))).astype(jnp.bfloat16)

def resnet_block(seq, arrived, swapped, g1, w1, b1, g2, w2, b2, ga, wq, bq, wk, cols):
    total, p_out, c = seq.shape
    frame_count = total // 2
    vm = pl.BlockSpec(memory_space=pltpu.VMEM)
    return pl.pallas_call(
        functools.partial(block_kernel, cols, frame_count),
        out_shape=(jax.ShapeDtypeStruct((frame_count, p_out, c), jnp.float32),
                   jax.ShapeDtypeStruct((frame_count, p_out, c), jnp.bfloat16),
                   jax.ShapeDtypeStruct((frame_count, p_out, c), jnp.bfloat16)),
        in_specs=[vm] * 13,
        out_specs=(vm, vm, vm),
    )(seq, arrived, swapped, g1.reshape(1, c), w1.reshape(27, c, c), b1.reshape(1, c), g2.reshape(1, c),
      w2.reshape(27, c, c), b2.reshape(1, c), ga.reshape(1, c), wq, bq.reshape(1, c), wk)


def local(
    frames,
    norm1_gain,
    conv1_weight,
    conv1_bias,
    norm2_gain,
    conv2_weight,
    conv2_bias,
    attn_gain,
    w_query,
    b_query,
    w_key,
    w_value,
    b_value,
    w_out,
    b_out,
):
    own = with_layout_constraint(frames[:, 0], Layout(major_to_minor=(0, 1, 2, 3)))
    frame_count, row_count, col_count, channels = own.shape
    inner = lax.axis_size("inner")
    bands = lax.axis_size("outer") * inner
    band = lax.axis_index("outer") * inner + lax.axis_index("inner")
    is_first = lax.axis_index("tm") == 0
    height = bands * row_count

    partner = lax.ppermute(own, "tm", [(0, 1), (1, 0)])
    even = jnp.where(is_first, own, partner)
    odd = jnp.where(is_first, partner, own)
    seq = jnp.stack([even, odd], axis=1).reshape(2 * frame_count, row_count, col_count, channels)

    up = [(2 * i, 2 * i + 2) for i in range(bands - 1)]
    down = [(2 * i + 3, 2 * i + 1) for i in range(bands - 1)]
    edge = jnp.where(is_first, seq[:, row_count - HALO :], seq[:, :HALO])
    arrived = lax.ppermute(edge, ("outer", "inner", "tm"), up + down)
    swapped = lax.ppermute(arrived, "tm", [(0, 1), (1, 0)])

    token_count = row_count * col_count
    residual, normed, folded = resnet_block(
        seq.reshape(2 * frame_count, -1, channels),
        arrived.reshape(2 * frame_count, -1, channels),
        swapped.reshape(2 * frame_count, -1, channels),
        norm1_gain,
        conv1_weight,
        conv1_bias,
        norm2_gain,
        conv2_weight,
        conv2_bias,
        attn_gain,
        w_query,
        b_query,
        w_key,
        col_count,
    )
    normed = normed.reshape(frame_count, row_count, col_count, channels)
    folded = folded.reshape(frame_count, token_count, channels)

    swap = [(0, 1), (1, 0)]
    partner_queries = lax.ppermute(folded, "inner", swap)
    spans = lax.axis_size("outer")
    if spans <= 4:
        shares = [normed] + [
            lax.ppermute(normed, "outer", [(i, (i + k) % spans) for i in range(spans)])
            for k in range(1, spans)
        ]
    else:
        shares = [lax.all_gather(normed, "outer", axis=1, tiled=True)]
    shares = [share.reshape(frame_count, -1, channels) for share in shares]
    def partial(queries):
        scores = [
            jnp.einsum("fqc,fkc->fqk", queries, share, preferred_element_type=jnp.float32)
            for share in shares
        ]
        top = functools.reduce(jnp.maximum, [jnp.max(x, axis=-1, keepdims=True) for x in scores])
        weights = [jnp.exp(x - top) for x in scores]
        total = sum(jnp.sum(w, axis=-1, keepdims=True) for w in weights)
        accum = sum(
            jnp.einsum(
                "fqk,fkc->fqc", w.astype(jnp.bfloat16), share, preferred_element_type=jnp.float32
            )
            for w, share in zip(weights, shares)
        )
        return accum, jnp.concatenate([top, total], axis=-1)

    back_accum, back_stats = partial(partner_queries)
    parts = []
    rest = back_stats
    for _ in range(3):
        head = lax.reduce_precision(rest, exponent_bits=8, mantissa_bits=7)
        parts.append(head)
        rest = rest - head
    packed = jnp.concatenate([back_accum] + parts, axis=-1).astype(jnp.bfloat16)
    returned = lax.ppermute(packed, "inner", swap).astype(jnp.float32)
    returned_accum = returned[..., :channels]
    pieces = [returned[..., channels + 2 * i : channels + 2 * i + 2] for i in range(3)]
    returned_stats = pieces[0] + (pieces[1] + pieces[2])
    mine_accum, mine_stats = partial(folded)
    top_mine = mine_stats[..., :1]
    top_back = returned_stats[..., :1]
    highest = jnp.maximum(top_mine, top_back)
    scale_mine = jnp.exp(top_mine - highest)
    scale_back = jnp.exp(top_back - highest)
    total = mine_stats[..., 1:] * scale_mine + returned_stats[..., 1:] * scale_back
    accum = mine_accum * scale_mine + returned_accum * scale_back
    mixed = (accum / total).astype(jnp.bfloat16).reshape(-1, channels)
    value = (jnp.dot(mixed, w_value, preferred_element_type=jnp.float32) + b_value).astype(
        jnp.bfloat16
    )
    decoded = (
        residual.reshape(-1, channels)
        + jnp.dot(value, w_out, preferred_element_type=jnp.float32)
        + b_out
    )
    return decoded.reshape(frame_count, 1, row_count, col_count, channels)


def solution(mesh):
    clips, bands, cores = mesh.devices.shape
    split = jax.sharding.Mesh(
        mesh.devices.reshape(clips, bands // 2, 2, cores), ("clips", "outer", "inner", "tm")
    )
    banded = P("clips", "tm", ("outer", "inner"), None, None)
    placed = (banded,) + (P(),) * 14
    return jax.shard_map(
        local,
        mesh=split,
        in_specs=placed,
        out_specs=banded,
        check_vma=False,
    )
```

```python
import functools
import math

import jax
import jax.numpy as jnp
from jax import lax
from jax.experimental import pallas as pl
from jax.experimental.layout import Layout, with_layout_constraint
from jax.experimental.pallas import tpu as pltpu
from jax.sharding import PartitionSpec as P

epsilon = 1e-06
HALO = 2


def rms_scale(values, gain):
    return values * lax.rsqrt(jnp.mean(values * values, axis=-1, keepdims=True) + epsilon) * gain


def conv_rows(source, taps):
    return lax.conv_general_dilated(
        source,
        taps,
        window_strides=(1, 1),
        padding=((0, 0), (1, 1)),
        dimension_numbers=("NHWC", "HWIO", "NHWC"),
        preferred_element_type=jnp.float32,
    )


def causal_time_conv(seq, weight):
    frame_total = seq.shape[0]
    out = None
    for p in range(3):
        lag = 2 - p
        if lag >= frame_total:
            continue
        part = conv_rows(seq[: frame_total - lag], weight[p])
        if lag:
            part = jnp.pad(part, ((lag, 0), (0, 0), (0, 0), (0, 0)))
        out = part if out is None else out + part
    return out


def _rms(v, g):
    return v * lax.rsqrt(jnp.mean(v * v, axis=-1, keepdims=True) + epsilon) * g

def _silu(v):
    return v * (1.0 / (1.0 + jnp.exp(-v)))

def block_kernel(cols, frame_count, own_ref, partner_ref, arrived_ref, swapped_ref, g1_ref, w1_ref, b1_ref, g2_ref,
                 w2_ref, b2_ref, ga_ref, wq_ref, bq_ref, wk_ref, res_ref, normed_ref, folded_ref):
    total = 2 * frame_count
    p_out = own_ref.shape[1]
    p_mid = p_out + 2 * cols
    first = lax.axis_index("tm") == 0

    def band_of(t):
        mine, other = own_ref[t // 2], partner_ref[t // 2]
        return jnp.where(first, mine, other) if t % 2 == 0 else jnp.where(first, other, mine)

    def extended(t):
        above = jnp.where(first, arrived_ref[t], swapped_ref[t])
        below = jnp.where(first, swapped_ref[t], arrived_ref[t])
        return jnp.concatenate([above, band_of(t), below], axis=0)

    def shifted(a):
        n = a.shape[0]
        col = lax.broadcasted_iota(jnp.int32, (n, 1), 0) % cols
        left = jnp.where(col == 0, 0.0, pltpu.roll(a, 1, 0))
        right = jnp.where(col == cols - 1, 0.0, pltpu.roll(a, n - 1, 0))
        return [left.astype(jnp.bfloat16), a.astype(jnp.bfloat16), right.astype(jnp.bfloat16)]

    def conv_frame(sources, w_ref, out_rows):
        acc = None
        for p, trip in enumerate(sources):
            if trip is None:
                continue
            for q in range(3):
                for s in range(3):
                    window = trip[s][q * cols: q * cols + out_rows]
                    part = jnp.dot(window, w_ref[(p * 3 + q) * 3 + s], preferred_element_type=jnp.float32)
                    acc = part if acc is None else acc + part
        return acc

    g1 = g1_ref[...]
    act1 = [shifted(_silu(_rms(extended(t).astype(jnp.float32), g1)).astype(jnp.bfloat16).astype(jnp.float32)) for t in range(total)]
    inner = lax.axis_size("inner")
    band = lax.axis_index("outer") * inner + lax.axis_index("inner")
    band_rows = p_out // cols
    height = lax.axis_size("outer") * inner * band_rows
    lo = 1 - band * band_rows
    hi = height - band * band_rows + 1
    row = lax.broadcasted_iota(jnp.int32, (p_mid, 1), 0) // cols
    inside = (row >= lo) & (row < hi)
    g2 = g2_ref[...]
    b1 = b1_ref[...]
    act2 = []
    for j in range(total):
        srcs = [act1[j + p - 2] if j + p - 2 >= 0 else None for p in range(3)]
        out1 = conv_frame(srcs, w1_ref, p_mid) + b1
        act2.append(jnp.where(inside, _silu(_rms(out1, g2)), 0.0).astype(jnp.bfloat16).astype(jnp.float32))
    b2 = b2_ref[...]
    ga = ga_ref[...]
    zero = None
    for k in range(frame_count):
        def pick(t_even):
            a = act2[t_even] if 0 <= t_even < total else None
            b = act2[t_even + 1] if 0 <= t_even + 1 < total else None
            if a is None and b is None:
                return None
            a = jnp.zeros_like(act2[0]) if a is None else a
            b = jnp.zeros_like(act2[0]) if b is None else b
            return shifted(jnp.where(first, a, b))
        srcs = [pick(2 * k - 2), pick(2 * k - 1), pick(2 * k)]
        out2 = conv_frame(srcs, w2_ref, p_out) + b2
        res = own_ref[k].astype(jnp.float32) + out2
        res_ref[k] = res
        normed = _rms(res, ga).astype(jnp.bfloat16)
        normed_ref[k] = normed
        query = jnp.dot(normed, wq_ref[...], preferred_element_type=jnp.float32) + bq_ref[...]
        folded = lax.dot_general(
            query.astype(jnp.bfloat16), wk_ref[...], (((1,), (1,)), ((), ())),
            preferred_element_type=jnp.float32,
        )
        folded_ref[k] = (folded * (1.0 / math.sqrt(res.shape[-1]))).astype(jnp.bfloat16)

def resnet_block(own, partner, arrived, swapped, g1, w1, b1, g2, w2, b2, ga, wq, bq, wk, cols):
    frame_count, p_out, c = own.shape
    vm = pl.BlockSpec(memory_space=pltpu.VMEM)
    return pl.pallas_call(
        functools.partial(block_kernel, cols, frame_count),
        out_shape=(jax.ShapeDtypeStruct((frame_count, p_out, c), jnp.float32),
                   jax.ShapeDtypeStruct((frame_count, p_out, c), jnp.bfloat16),
                   jax.ShapeDtypeStruct((frame_count, p_out, c), jnp.bfloat16)),
        in_specs=[vm] * 14,
        out_specs=(vm, vm, vm),
    )(own, partner, arrived, swapped, g1.reshape(1, c), w1.reshape(27, c, c), b1.reshape(1, c), g2.reshape(1, c),
      w2.reshape(27, c, c), b2.reshape(1, c), ga.reshape(1, c), wq, bq.reshape(1, c), wk)


def local(
    frames,
    norm1_gain,
    conv1_weight,
    conv1_bias,
    norm2_gain,
    conv2_weight,
    conv2_bias,
    attn_gain,
    w_query,
    b_query,
    w_key,
    w_value,
    b_value,
    w_out,
    b_out,
):
    own = with_layout_constraint(frames[:, 0], Layout(major_to_minor=(0, 1, 2, 3)))
    frame_count, row_count, col_count, channels = own.shape
    inner = lax.axis_size("inner")
    bands = lax.axis_size("outer") * inner
    band = lax.axis_index("outer") * inner + lax.axis_index("inner")
    is_first = lax.axis_index("tm") == 0
    height = bands * row_count

    partner = lax.ppermute(own, "tm", [(0, 1), (1, 0)])
    even = jnp.where(is_first, own, partner)
    odd = jnp.where(is_first, partner, own)
    seq = jnp.stack([even, odd], axis=1).reshape(2 * frame_count, row_count, col_count, channels)

    up = [(2 * i, 2 * i + 2) for i in range(bands - 1)]
    down = [(2 * i + 3, 2 * i + 1) for i in range(bands - 1)]
    edge = jnp.where(is_first, seq[:, row_count - HALO :], seq[:, :HALO])
    arrived = lax.ppermute(edge, ("outer", "inner", "tm"), up + down)
    swapped = lax.ppermute(arrived, "tm", [(0, 1), (1, 0)])

    token_count = row_count * col_count
    residual, normed, folded = resnet_block(
        own.reshape(frame_count, -1, channels),
        partner.reshape(frame_count, -1, channels),
        arrived.reshape(2 * frame_count, -1, channels),
        swapped.reshape(2 * frame_count, -1, channels),
        norm1_gain,
        conv1_weight,
        conv1_bias,
        norm2_gain,
        conv2_weight,
        conv2_bias,
        attn_gain,
        w_query,
        b_query,
        w_key,
        col_count,
    )
    normed = normed.reshape(frame_count, row_count, col_count, channels)
    folded = folded.reshape(frame_count, token_count, channels)

    swap = [(0, 1), (1, 0)]
    partner_queries = lax.ppermute(folded, "inner", swap)
    spans = lax.axis_size("outer")
    if spans <= 4:
        shares = [normed] + [
            lax.ppermute(normed, "outer", [(i, (i + k) % spans) for i in range(spans)])
            for k in range(1, spans)
        ]
        keys = jnp.concatenate(shares, axis=1)
    else:
        keys = lax.all_gather(normed, "outer", axis=1, tiled=True)
    keys = keys.reshape(frame_count, -1, channels)
    def partial(queries):
        scores = jnp.einsum("fqc,fkc->fqk", queries, keys, preferred_element_type=jnp.float32)
        top = jnp.max(scores, axis=-1, keepdims=True)
        weights = jnp.exp(scores - top)
        total = jnp.sum(weights, axis=-1, keepdims=True)
        accum = jnp.einsum(
            "fqk,fkc->fqc", weights.astype(jnp.bfloat16), keys, preferred_element_type=jnp.float32
        )
        return accum, jnp.concatenate([top, total], axis=-1)

    back_accum, back_stats = partial(partner_queries)
    parts = []
    rest = back_stats
    for _ in range(3):
        head = lax.reduce_precision(rest, exponent_bits=8, mantissa_bits=7)
        parts.append(head)
        rest = rest - head
    packed = jnp.concatenate([back_accum] + parts, axis=-1).astype(jnp.bfloat16)
    returned = lax.ppermute(packed, "inner", swap).astype(jnp.float32)
    returned_accum = returned[..., :channels]
    pieces = [returned[..., channels + 2 * i : channels + 2 * i + 2] for i in range(3)]
    returned_stats = pieces[0] + (pieces[1] + pieces[2])
    mine_accum, mine_stats = partial(folded)
    top_mine = mine_stats[..., :1]
    top_back = returned_stats[..., :1]
    highest = jnp.maximum(top_mine, top_back)
    scale_mine = jnp.exp(top_mine - highest)
    scale_back = jnp.exp(top_back - highest)
    total = mine_stats[..., 1:] * scale_mine + returned_stats[..., 1:] * scale_back
    accum = mine_accum * scale_mine + returned_accum * scale_back
    mixed = (accum / total).astype(jnp.bfloat16).reshape(-1, channels)
    value = (jnp.dot(mixed, w_value, preferred_element_type=jnp.float32) + b_value).astype(
        jnp.bfloat16
    )
    decoded = (
        residual.reshape(-1, channels)
        + jnp.dot(value, w_out, preferred_element_type=jnp.float32)
        + b_out
    )
    return decoded.reshape(frame_count, 1, row_count, col_count, channels)


def solution(mesh):
    clips, bands, cores = mesh.devices.shape
    split = jax.sharding.Mesh(
        mesh.devices.reshape(clips, bands // 2, 2, cores), ("clips", "outer", "inner", "tm")
    )
    banded = P("clips", "tm", ("outer", "inner"), None, None)
    placed = (banded,) + (P(),) * 14
    return jax.shard_map(
        local,
        mesh=split,
        in_specs=placed,
        out_specs=banded,
        check_vma=False,
    )
```

```python
import functools
import math

import jax
import jax.numpy as jnp
from jax import lax
from jax.experimental import pallas as pl
from jax.experimental.layout import Layout, with_layout_constraint
from jax.experimental.pallas import tpu as pltpu
from jax.sharding import PartitionSpec as P

epsilon = 1e-06
HALO = 2


def rms_scale(values, gain):
    return values * lax.rsqrt(jnp.mean(values * values, axis=-1, keepdims=True) + epsilon) * gain


def conv_rows(source, taps):
    return lax.conv_general_dilated(
        source,
        taps,
        window_strides=(1, 1),
        padding=((0, 0), (1, 1)),
        dimension_numbers=("NHWC", "HWIO", "NHWC"),
        preferred_element_type=jnp.float32,
    )


def causal_time_conv(seq, weight):
    frame_total = seq.shape[0]
    out = None
    for p in range(3):
        lag = 2 - p
        if lag >= frame_total:
            continue
        part = conv_rows(seq[: frame_total - lag], weight[p])
        if lag:
            part = jnp.pad(part, ((lag, 0), (0, 0), (0, 0), (0, 0)))
        out = part if out is None else out + part
    return out


def _rms(v, g):
    return v * lax.rsqrt(jnp.mean(v * v, axis=-1, keepdims=True) + epsilon) * g

def _silu(v):
    return v * (1.0 / (1.0 + jnp.exp(-v)))

def block_kernel(cols, frame_count, seq_ref, arrived_ref, swapped_ref, g1_ref, w1_ref, b1_ref, g2_ref,
                 w2_ref, b2_ref, ga_ref, wq_ref, bq_ref, wk_ref, res_ref, normed_ref, folded_ref):
    total = 2 * frame_count
    p_out = seq_ref.shape[1]
    p_mid = p_out + 2 * cols
    first = lax.axis_index("tm") == 0

    def extended(t):
        above = jnp.where(first, arrived_ref[t], swapped_ref[t])
        below = jnp.where(first, swapped_ref[t], arrived_ref[t])
        return jnp.concatenate([above, seq_ref[t], below], axis=0)

    def shifted(a):
        n = a.shape[0]
        col = lax.broadcasted_iota(jnp.int32, (n, 1), 0) % cols
        left = jnp.where(col == 0, 0.0, pltpu.roll(a, 1, 0))
        right = jnp.where(col == cols - 1, 0.0, pltpu.roll(a, n - 1, 0))
        return [left.astype(jnp.bfloat16), a.astype(jnp.bfloat16), right.astype(jnp.bfloat16)]

    def conv_frame(sources, w_ref, out_rows):
        acc = None
        for p, trip in enumerate(sources):
            if trip is None:
                continue
            for q in range(3):
                for s in range(3):
                    window = trip[s][q * cols: q * cols + out_rows]
                    part = jnp.dot(window, w_ref[(p * 3 + q) * 3 + s], preferred_element_type=jnp.float32)
                    acc = part if acc is None else acc + part
        return acc

    g1 = g1_ref[...]
    act1 = [shifted(_silu(_rms(extended(t).astype(jnp.float32), g1)).astype(jnp.bfloat16).astype(jnp.float32)) for t in range(total)]
    inner = lax.axis_size("inner")
    band = lax.axis_index("outer") * inner + lax.axis_index("inner")
    band_rows = p_out // cols
    height = lax.axis_size("outer") * inner * band_rows
    lo = 1 - band * band_rows
    hi = height - band * band_rows + 1
    row = lax.broadcasted_iota(jnp.int32, (p_mid, 1), 0) // cols
    inside = (row >= lo) & (row < hi)
    g2 = g2_ref[...]
    b1 = b1_ref[...]
    act2 = []
    for j in range(total):
        srcs = [act1[j + p - 2] if j + p - 2 >= 0 else None for p in range(3)]
        out1 = conv_frame(srcs, w1_ref, p_mid) + b1
        act2.append(jnp.where(inside, _silu(_rms(out1, g2)), 0.0).astype(jnp.bfloat16).astype(jnp.float32))
    b2 = b2_ref[...]
    ga = ga_ref[...]
    zero = None
    for k in range(frame_count):
        def pick(t_even):
            a = act2[t_even] if 0 <= t_even < total else None
            b = act2[t_even + 1] if 0 <= t_even + 1 < total else None
            if a is None and b is None:
                return None
            a = jnp.zeros_like(act2[0]) if a is None else a
            b = jnp.zeros_like(act2[0]) if b is None else b
            return shifted(jnp.where(first, a, b))
        srcs = [pick(2 * k - 2), pick(2 * k - 1), pick(2 * k)]
        out2 = conv_frame(srcs, w2_ref, p_out) + b2
        own = jnp.where(first, seq_ref[2 * k], seq_ref[2 * k + 1])
        res = own.astype(jnp.float32) + out2
        res_ref[k] = res
        normed = _rms(res, ga).astype(jnp.bfloat16)
        normed_ref[k] = normed
        query = jnp.dot(normed, wq_ref[...], preferred_element_type=jnp.float32) + bq_ref[...]
        folded = lax.dot_general(
            query.astype(jnp.bfloat16), wk_ref[...], (((1,), (1,)), ((), ())),
            preferred_element_type=jnp.float32,
        )
        folded_ref[k] = (folded * (1.0 / math.sqrt(res.shape[-1]))).astype(jnp.bfloat16)

def resnet_block(seq, arrived, swapped, g1, w1, b1, g2, w2, b2, ga, wq, bq, wk, cols):
    total, p_out, c = seq.shape
    frame_count = total // 2
    vm = pl.BlockSpec(memory_space=pltpu.VMEM)
    return pl.pallas_call(
        functools.partial(block_kernel, cols, frame_count),
        out_shape=(jax.ShapeDtypeStruct((frame_count, p_out, c), jnp.float32),
                   jax.ShapeDtypeStruct((frame_count, p_out, c), jnp.bfloat16),
                   jax.ShapeDtypeStruct((frame_count, p_out, c), jnp.bfloat16)),
        in_specs=[vm] * 13,
        out_specs=(vm, vm, vm),
    )(seq, arrived, swapped, g1.reshape(1, c), w1.reshape(27, c, c), b1.reshape(1, c), g2.reshape(1, c),
      w2.reshape(27, c, c), b2.reshape(1, c), ga.reshape(1, c), wq, bq.reshape(1, c), wk)


def local(
    frames,
    norm1_gain,
    conv1_weight,
    conv1_bias,
    norm2_gain,
    conv2_weight,
    conv2_bias,
    attn_gain,
    w_query,
    b_query,
    w_key,
    w_value,
    b_value,
    w_out,
    b_out,
):
    own = with_layout_constraint(frames[:, 0], Layout(major_to_minor=(0, 1, 2, 3)))
    frame_count, row_count, col_count, channels = own.shape
    inner = lax.axis_size("inner")
    bands = lax.axis_size("outer") * inner
    band = lax.axis_index("outer") * inner + lax.axis_index("inner")
    is_first = lax.axis_index("tm") == 0
    height = bands * row_count

    partner = lax.ppermute(own, "tm", [(0, 1), (1, 0)])
    even = jnp.where(is_first, own, partner)
    odd = jnp.where(is_first, partner, own)
    seq = jnp.stack([even, odd], axis=1).reshape(2 * frame_count, row_count, col_count, channels)

    up = [(2 * i, 2 * i + 2) for i in range(bands - 1)]
    down = [(2 * i + 3, 2 * i + 1) for i in range(bands - 1)]
    edge = jnp.where(is_first, seq[:, row_count - HALO :], seq[:, :HALO])
    arrived = lax.ppermute(edge, ("outer", "inner", "tm"), up + down)
    swapped = lax.ppermute(arrived, "tm", [(0, 1), (1, 0)])

    token_count = row_count * col_count
    residual, normed, folded = resnet_block(
        seq.reshape(2 * frame_count, -1, channels),
        arrived.reshape(2 * frame_count, -1, channels),
        swapped.reshape(2 * frame_count, -1, channels),
        norm1_gain,
        conv1_weight,
        conv1_bias,
        norm2_gain,
        conv2_weight,
        conv2_bias,
        attn_gain,
        w_query,
        b_query,
        w_key,
        col_count,
    )
    normed = normed.reshape(frame_count, row_count, col_count, channels)
    folded = folded.reshape(frame_count, token_count, channels)

    swap = [(0, 1), (1, 0)]
    partner_queries = lax.ppermute(folded, "inner", swap)
    spans = lax.axis_size("outer")
    if spans <= 4:
        shares = [normed] + [
            lax.ppermute(normed, "outer", [(i, (i + k) % spans) for i in range(spans)])
            for k in range(1, spans)
        ]
        keys = jnp.concatenate(shares, axis=1)
    else:
        keys = lax.all_gather(normed, "outer", axis=1, tiled=True)
    keys = keys.reshape(frame_count, -1, channels)
    def partial(queries):
        scores = jnp.einsum("fqc,fkc->fqk", queries, keys, preferred_element_type=jnp.float32)
        top = jnp.max(scores, axis=-1, keepdims=True)
        weights = jnp.exp(scores - top)
        total = jnp.sum(weights, axis=-1, keepdims=True)
        accum = jnp.einsum(
            "fqk,fkc->fqc", weights.astype(jnp.bfloat16), keys, preferred_element_type=jnp.float32
        )
        return accum, jnp.concatenate([top, total], axis=-1)

    back_accum, back_stats = partial(partner_queries)
    parts = []
    rest = back_stats
    for _ in range(3):
        head = lax.reduce_precision(rest, exponent_bits=8, mantissa_bits=7)
        parts.append(head)
        rest = rest - head
    packed = jnp.concatenate([back_accum] + parts, axis=-1).astype(jnp.bfloat16)
    returned = lax.ppermute(packed, "inner", swap).astype(jnp.float32)
    returned_accum = returned[..., :channels]
    pieces = [returned[..., channels + 2 * i : channels + 2 * i + 2] for i in range(3)]
    returned_stats = pieces[0] + (pieces[1] + pieces[2])
    mine_accum, mine_stats = partial(folded)
    top_mine = mine_stats[..., :1]
    top_back = returned_stats[..., :1]
    highest = jnp.maximum(top_mine, top_back)
    scale_mine = jnp.exp(top_mine - highest)
    scale_back = jnp.exp(top_back - highest)
    total = mine_stats[..., 1:] * scale_mine + returned_stats[..., 1:] * scale_back
    accum = mine_accum * scale_mine + returned_accum * scale_back
    mixed = (accum / total).astype(jnp.bfloat16).reshape(-1, channels)
    value = (jnp.dot(mixed, w_value, preferred_element_type=jnp.float32) + b_value).astype(
        jnp.bfloat16
    )
    shape = (frame_count * row_count, col_count, channels)
    projected = jnp.einsum(
        "rwc,cd->rdw", value.reshape(shape), w_out, preferred_element_type=jnp.float32
    )
    decoded = (
        jnp.swapaxes(residual.reshape(shape), 1, 2) + projected + b_out[None, :, None]
    )
    decoded = jnp.swapaxes(decoded, 1, 2)
    return decoded.reshape(frame_count, 1, row_count, col_count, channels)


def solution(mesh):
    clips, bands, cores = mesh.devices.shape
    split = jax.sharding.Mesh(
        mesh.devices.reshape(clips, bands // 2, 2, cores), ("clips", "outer", "inner", "tm")
    )
    banded = P("clips", "tm", ("outer", "inner"), None, None)
    placed = (banded,) + (P(),) * 14
    return jax.shard_map(
        local,
        mesh=split,
        in_specs=placed,
        out_specs=banded,
        check_vma=False,
    )
```
